32 devices in a mesh: seq: 8 (over y, x, core), tp: 4 (over z).
Axes of the slice: x: 2, y: 2, z: 4, core: 2. Of those that a mesh axis runs over, the one named last changes fastest.
Arguments:
- hidden: bfloat16 [1024, 8192], P('seq'), may hold values from -7 to 7
- norm_gain: bfloat16 [8192], replicated, may hold values from 0.099609375 to 1.8984375
- w_query: bfloat16 [8192, 1024], P('seq', 'tp'), may hold values from -1 to 1
- w_key: bfloat16 [8192, 128], P('seq'), may hold values from -64 to 64
- w_value: bfloat16 [8192, 128], P('seq'), may hold values from -0.0625 to 0.0625
- doc_lengths: int32 [8], replicated, may hold values from 1 to 640, 1024 in all
- critic_up: bfloat16 [8192, 4608], P('seq', 'tp'), may hold values from -0.0625 to 0.0625
- critic_down: bfloat16 [4, 4608, 8192], P(None, 'tp', 'seq'), may hold values from -0.09375 to 0.09375
- rule_ids: int32 [8], replicated, may hold values from 0 to 3
Outputs:
- attention: bfloat16 [1024, 1024], P('seq', 'tp')
- critic_values: bfloat16 [8, 8192], P(None, 'seq')
The draws below stay inside these ranges and needn't reach their ends.
Inputs may be any that keep to these rules, and one draw needn't show every extreme that they name: `doc_lengths`: the 8 lengths sum to 1024; the longest is exactly 640.
All inputs are finite; a program needn't handle non-finite values.
Results may differ from the reference program's by a relative error of at most 0.03.
The reference program's roundings to bfloat16 on the way (of `normed`, `end_rows` and `critic_hidden`) count: a program that leaves them out, or rounds other values in their place, can miss the bound.
Values may be sent and summed in bfloat16 or wider, within the bound.
No kernel may reach another device: no remote copies, remote signals or barrier semaphores. Data moves between devices by JAX's collectives and lax.ppermute only.
A program may use at most 64 MiB of HBM per device.

```python
import math
import jax
import jax.numpy as jnp
import numpy as np
from jax import lax

D = 8192
HEAD = 128
GROUP = 8
DOCS = 8
RULES = 4
LEN = 1024
HEADS = 8
KV_HEADS = 1
CF = 4608


def query_table(key):
    base = jax.random.normal(jax.random.fold_in(key, 11), (D, HEADS * HEAD), jnp.float32)
    return jnp.clip(base, -4.0, 4.0) * (1.0 / math.sqrt(D))


def draw_w_query(key, part):
    return query_table(key).astype(jnp.bfloat16)


def draw_w_key(key, part):
    own = jax.random.normal(jax.random.fold_in(key, 12), (D, KV_HEADS * HEAD), jnp.float32)
    result = jnp.clip(own, -4.0, 4.0) * (1.0 / math.sqrt(D))
    return result.astype(jnp.bfloat16)


def draw_hidden(key, part):
    base = jnp.clip(jax.random.normal(jax.random.fold_in(key, 21), (LEN, D), jnp.float32), -6.0, 6.0)
    return base.astype(jnp.bfloat16)


def with_ends(values, own_key, least, largest):
    dims = values.shape
    spot = [jax.random.randint(jax.random.fold_in(own_key, axis), (), 0, dims[axis]) for axis in range(len(dims))]
    values = values.at[tuple(spot)].set(least)
    longest = dims.index(max(dims))
    spot[longest] = (spot[longest] + 1) % dims[longest]
    return values.at[tuple(spot)].set(largest)


def levels(key, shape, pieces, smallest, high):
    def one(axis_at, blocks):
        steps = jax.random.uniform(jax.random.fold_in(jax.random.fold_in(key, 6), axis_at), (blocks,), jnp.float32, smallest / len(pieces), high / len(pieces))
        return jnp.repeat(jnp.exp(steps), shape[axis_at] // blocks).reshape((-1,) + (1,) * (len(shape) - axis_at - 1))

    factor_of = one(*pieces[0])
    for cut in pieces[1:]:
        factor_of = factor_of * one(*cut)
    return factor_of


def split_up(number_of, total, limit, lean):
    weights = [(1 << 20) // math.isqrt(standing ** lean) + 1 for standing in range(2, number_of + 1)]
    spare, counts = total - limit - (number_of - 1), [1] * (number_of - 1)
    while spare > 0:
        candidates = [i for i in range(number_of - 1) if counts[i] < limit]
        pool, budget = sum([weights[i] for i in candidates]), spare
        for i in candidates:
            more = min(limit - counts[i], max(1, budget * weights[i] // pool), spare)
            counts[i] = counts[i] + more
            spare = spare - more
    return np.array([limit] + counts)


def ragged(rng, number_of, total, most, slope):
    if number_of == 2:
        one = jax.random.randint(rng, (), max(1, total - most), min(most, total - 1) + 1)
        return jnp.stack([one, total - one])
    tallies = jnp.asarray(split_up(number_of, total, most, slope), jnp.int32)
    pairs = (number_of - 1) // 2
    giver, taker = tallies[1:1 + 2 * pairs:2], tallies[2:2 + 2 * pairs:2]
    slack = jnp.minimum(giver - 1, most - taker)
    passed = jax.random.randint(jax.random.fold_in(rng, 1), (pairs,), 0, 1 << 20) % (slack + 1)
    tallies = tallies.at[1:1 + 2 * pairs:2].set(giver - passed).at[2:2 + 2 * pairs:2].set(taker + passed)
    return tallies[jax.random.permutation(jax.random.fold_in(rng, 2), number_of)]


def normal_values(rng, shape, scale, most, cuts=(), held_as=jnp.bfloat16):
    values = scale * jax.random.normal(rng, shape, jnp.float32)
    if cuts:
        values = values * levels(rng, shape, cuts, -0.22, 0.18)
    return jnp.clip(values, -most, most).astype(held_as)


def setup_inputs(seed: int = 0) -> dict:
    streams_of = jax.random.split(jax.random.key(seed), 10)
    hidden = draw_hidden(jax.random.fold_in(streams_of[9], 71), 0)
    norm_gain = jnp.clip(1.0 + 0.18 * jax.random.normal(streams_of[1], (D,), jnp.float32), 0.099609375, 1.8984375).astype(jnp.bfloat16)
    w_query = draw_w_query(jax.random.fold_in(streams_of[9], 71), 0)
    w_key = draw_w_key(jax.random.fold_in(streams_of[9], 71), 0)
    w_value = normal_values(streams_of[4], (D, KV_HEADS * HEAD), D ** -0.5, 0.0625, ((0, 8),))
    doc_lengths = ragged(streams_of[5], DOCS, LEN, LEN // 2 + LEN // 8, 2).astype(jnp.int32)
    critic_up = normal_values(streams_of[6], (D, CF), D ** -0.5, 0.0625, ((0, 8), (1, 4)))
    critic_down = normal_values(streams_of[7], (RULES, CF, D), CF ** -0.5, 0.09375, ((1, 4), (2, 8)))
    rule_ids = with_ends(jax.random.randint(streams_of[8], (DOCS,), 0, RULES), jax.random.fold_in(streams_of[8], 1), 0, RULES - 1).astype(jnp.int32)
    return dict(hidden=hidden, norm_gain=norm_gain, w_query=w_query, w_key=w_key, w_value=w_value, doc_lengths=doc_lengths, critic_up=critic_up, critic_down=critic_down, rule_ids=rule_ids)


def rms_norm(values, norm_gain):
    widened = values.astype(jnp.float32)
    mean_square = lax.optimization_barrier(jnp.mean(widened * widened, axis=-1, keepdims=True))
    return (widened * lax.rsqrt(mean_square + 1e-05) * norm_gain.astype(jnp.float32)).astype(jnp.bfloat16)

def reference(hidden, norm_gain, w_query, w_key, w_value, doc_lengths, critic_up, critic_down, rule_ids):
    normed = rms_norm(hidden, norm_gain)
    queries = jnp.dot(normed, w_query, preferred_element_type=jnp.float32).astype(jnp.bfloat16).reshape(LEN, HEADS, HEAD)
    keys = jnp.dot(normed, w_key, preferred_element_type=jnp.float32).astype(jnp.bfloat16).reshape(LEN, KV_HEADS, HEAD)
    values = jnp.dot(normed, w_value, preferred_element_type=jnp.float32).astype(jnp.bfloat16).reshape(LEN, KV_HEADS, HEAD)
    doc_ends = (jnp.cumsum(doc_lengths) - 1).astype(jnp.int32)
    positions = jnp.arange(LEN, dtype=jnp.int32)
    segment = lax.optimization_barrier(jnp.sum((positions[:, None] > doc_ends[None, :]).astype(jnp.int32), axis=1))
    allowed = (segment[:, None] == segment[None, :]) & (positions[None, :] <= positions[:, None])
    inverse_root = 1.0 / math.sqrt(HEAD)

    def one_head(head):
        query_head = lax.dynamic_index_in_dim(queries, head, 1, keepdims=False)
        key_head = lax.dynamic_index_in_dim(keys, head // GROUP, 1, keepdims=False)
        value_head = lax.dynamic_index_in_dim(values, head // GROUP, 1, keepdims=False)
        scores = jnp.dot(query_head, key_head.T, preferred_element_type=jnp.float32) * inverse_root
        scores = jnp.where(allowed, scores, -1e+30)
        maxima = lax.optimization_barrier(jnp.max(scores, axis=1, keepdims=True))
        weights = jnp.where(allowed, jnp.exp(scores - maxima), 0.0)
        totals = lax.optimization_barrier(jnp.sum(weights, axis=1, keepdims=True))
        mixed = jnp.dot(weights.astype(jnp.bfloat16), value_head, preferred_element_type=jnp.float32)
        return mixed / totals
    heads_out = lax.map(one_head, jnp.arange(HEADS, dtype=jnp.int32))
    attention = jnp.transpose(heads_out, (1, 0, 2)).reshape(LEN, HEADS * HEAD).astype(jnp.bfloat16)
    end_rows = jnp.take(normed, doc_ends, axis=0)
    critic_hidden = jax.nn.silu(jnp.dot(end_rows, critic_up, preferred_element_type=jnp.float32)).astype(jnp.bfloat16)
    per_rule = jnp.einsum('dc,rce->dre', critic_hidden.astype(jnp.float32), critic_down.astype(jnp.float32))
    rule_pick = (rule_ids[:, None] == jnp.arange(RULES, dtype=jnp.int32)[None, :]).astype(jnp.float32)
    critic_values = jnp.einsum('dr,dre->de', rule_pick, per_rule).astype(jnp.bfloat16)
    return (attention, critic_values)
```

```python
import math

import jax
import jax.numpy as jnp
from jax import lax
from jax.sharding import PartitionSpec as P

HEAD = 128
GROUP = 8


def rms_norm(values, norm_gain):
    widened = values.astype(jnp.float32)
    mean_square = jnp.mean(widened * widened, axis=-1, keepdims=True)
    return (widened * lax.rsqrt(mean_square + 1e-05) * norm_gain.astype(jnp.float32)).astype(
        jnp.bfloat16
    )


def shifted(x, axis, n, k):
    return lax.ppermute(x, axis, [(j, (j + k) % n) for j in range(n)])


def group_shifted(x, axis, n, size, k):
    perm = [(j, j - j % size + (j % size + k) % size) for j in range(n)]
    return lax.ppermute(x, axis, perm)


def xor_perm(n, pick):
    return [(j, pick(j)) for j in range(n)]


def gather_pieces(blk, n):
    i = lax.axis_index("seq")
    rows = blk.shape[0]
    if n != 8:
        full = lax.all_gather(blk, "seq", axis=0, tiled=True)
        return [(full, jnp.int32(0), n * rows)]
    core = i % 2
    chip = i // 2
    sib = lax.ppermute(blk, "seq", xor_perm(8, lambda j: j ^ 1))
    pair = jnp.concatenate([blk, sib], axis=0)
    nb = lax.ppermute(pair, "seq", xor_perm(8, lambda j: j ^ 2 if j % 2 == 0 else j ^ 4))
    dg = lax.ppermute(nb[:rows], "seq", xor_perm(8, lambda j: j ^ 5 if j % 2 == 0 else j ^ 3))
    oth = lax.ppermute(jnp.concatenate([nb, dg], axis=0), "seq", xor_perm(8, lambda j: j ^ 1))
    nb_chip = chip ^ (1 + core)
    oth_chip = chip ^ (2 - core)
    diag = chip ^ 3
    return [
        (blk, i, rows),
        (sib, i ^ 1, rows),
        (nb[:rows], 2 * nb_chip + core, rows),
        (nb[rows:], 2 * nb_chip + 1 - core, rows),
        (dg, 2 * diag + 1 - core, rows),
        (oth[:rows], 2 * oth_chip + 1 - core, rows),
        (oth[rows : 2 * rows], 2 * oth_chip + core, rows),
        (oth[2 * rows :], 2 * diag + core, rows),
    ]


def project(normed, pieces):
    total = None
    for piece, source, rows in pieces:
        cols = lax.dynamic_slice_in_dim(normed, source * rows, rows, 1)
        term = jnp.dot(cols, piece, preferred_element_type=jnp.float32)
        total = term if total is None else total + term
    return total


def shards(
    hidden, norm_gain, w_query, w_key, w_value, doc_lengths, critic_up, critic_down, rule_ids
):
    n_seq = lax.axis_size("seq")
    n_tp = lax.axis_size("tp")
    seq_i = lax.axis_index("seq")
    tp_i = lax.axis_index("tp")
    normed = rms_norm(hidden, norm_gain)
    tokens_here = hidden.shape[0]
    d_rows = w_query.shape[0]
    heads_here = w_query.shape[1] // HEAD
    sharers = GROUP // heads_here
    kv_width = HEAD // sharers
    kv_head = tp_i * heads_here // GROUP
    kv_part = tp_i % sharers
    kv_start = kv_head * HEAD + kv_part * kv_width
    key_cols = lax.dynamic_slice_in_dim(w_key, kv_start, kv_width, 1)
    value_cols = lax.dynamic_slice_in_dim(w_value, kv_start, kv_width, 1)
    kv_weights = jnp.concatenate([key_cols, value_cols], axis=1)

    doc_ends = jnp.cumsum(doc_lengths) - 1
    first_row = seq_i * tokens_here
    query_pos = first_row + jnp.arange(tokens_here, dtype=jnp.int32)
    picker = (doc_ends[:, None] == query_pos[None, :]).astype(jnp.bfloat16)
    end_terms = jnp.dot(picker, normed, preferred_element_type=jnp.float32).astype(jnp.bfloat16)
    end_sum = lax.dynamic_slice_in_dim(end_terms, seq_i * d_rows, d_rows, 1).astype(jnp.float32)
    for k in range(1, n_seq):
        part = lax.dynamic_slice_in_dim(end_terms, ((seq_i + k) % n_seq) * d_rows, d_rows, 1)
        end_sum = end_sum + shifted(part, "seq", n_seq, k).astype(jnp.float32)
    end_rows = end_sum.astype(jnp.bfloat16)
    up_own = jnp.dot(end_rows, critic_up, preferred_element_type=jnp.float32)
    up_sum = up_own
    for k in range(1, n_seq):
        up_sum = up_sum + shifted(up_own, "seq", n_seq, k)
    critic_hidden = jax.nn.silu(up_sum).astype(jnp.bfloat16)
    per_rule = jnp.einsum(
        "dc,rce->dre", critic_hidden, critic_down, preferred_element_type=jnp.float32
    )
    rule_pick = rule_ids[:, None] == jnp.arange(critic_down.shape[0], dtype=jnp.int32)[None, :]
    chosen = jnp.sum(jnp.where(rule_pick[:, :, None], per_rule, 0.0), axis=1)
    if n_tp > 8:
        critic_sum = lax.psum(chosen, "tp")
    else:
        received = [chosen] + [shifted(chosen, "tp", n_tp, k) for k in range(1, n_tp)]
        critic_sum = None
        for m in range(n_tp):
            canon = received[0]
            for k in range(1, n_tp):
                canon = jnp.where((tp_i - k) % n_tp == m, received[k], canon)
            critic_sum = canon if critic_sum is None else critic_sum + canon
    critic_values = critic_sum.astype(jnp.bfloat16)

    kv_pieces = gather_pieces(kv_weights, n_seq)
    kv_own = project(normed, kv_pieces).astype(jnp.bfloat16)
    kv_got = [kv_own] + [group_shifted(kv_own, "tp", n_tp, sharers, k) for k in range(1, sharers)]
    key_parts, value_parts = [], []
    for m in range(sharers):
        canon = kv_got[0]
        for k in range(1, sharers):
            canon = jnp.where((kv_part - k) % sharers == m, kv_got[k], canon)
        key_parts.append(canon[:, :kv_width])
        value_parts.append(canon[:, kv_width:])
    kv_rows = jnp.concatenate(key_parts + value_parts, axis=1)
    kv_all = [kv_rows] + [shifted(kv_rows, "seq", n_seq, k) for k in range(1, n_seq)]
    key_block = jnp.concatenate([piece[:, :HEAD] for piece in kv_all], axis=0)
    value_block = jnp.concatenate([piece[:, HEAD:] for piece in kv_all], axis=0)
    key_pos = jnp.concatenate(
        [
            ((seq_i - k) % n_seq) * tokens_here + jnp.arange(tokens_here, dtype=jnp.int32)
            for k in range(n_seq)
        ]
    )

    q_pieces = gather_pieces(w_query, n_seq)
    queries = project(normed, q_pieces).astype(jnp.bfloat16).reshape(tokens_here, heads_here, HEAD)

    def segment_of(positions):
        return jnp.sum((positions[:, None] > doc_ends[None, :]).astype(jnp.int32), axis=1)

    query_seg = segment_of(query_pos)
    inverse_root = 1.0 / math.sqrt(HEAD)
    allowed = (query_seg[:, None] == segment_of(key_pos)[None, :]) & (
        key_pos[None, :] <= query_pos[:, None]
    )
    allowed = allowed[:, None, :]
    scores = (
        jnp.einsum("qhd,kd->qhk", queries, key_block, preferred_element_type=jnp.float32)
        * inverse_root
    )
    scores = jnp.where(allowed, scores, -1e30)
    maxima = jnp.max(scores, axis=2)
    expanded = jnp.where(allowed, jnp.exp(scores - maxima[:, :, None]), 0.0)
    totals = jnp.sum(expanded, axis=2)
    weighted = jnp.einsum(
        "qhk,kd->qhd",
        expanded.astype(jnp.bfloat16),
        value_block,
        preferred_element_type=jnp.float32,
    )
    attention = (
        (weighted / totals[:, :, None])
        .reshape(tokens_here, heads_here * HEAD)
        .astype(jnp.bfloat16)
    )
    return (attention, critic_values)


def solution(mesh):
    return jax.shard_map(
        shards,
        mesh=mesh,
        in_specs=(
            P("seq", None),
            P(),
            P("seq", "tp"),
            P("seq", None),
            P("seq", None),
            P(),
            P("seq", "tp"),
            P(None, "tp", "seq"),
            P(),
        ),
        out_specs=(P("seq", "tp"), P(None, "seq")),
        check_vma=False,
    )
```

```python
import math

import jax
import jax.numpy as jnp
from jax import lax
from jax.sharding import PartitionSpec as P

HEAD = 128
GROUP = 8


def rms_norm(values, norm_gain):
    widened = values.astype(jnp.float32)
    mean_square = jnp.mean(widened * widened, axis=-1, keepdims=True)
    return (widened * lax.rsqrt(mean_square + 1e-05) * norm_gain.astype(jnp.float32)).astype(
        jnp.bfloat16
    )


def xor_perm(n, pick):
    return [(j, pick(j)) for j in range(n)]


def xor_all_reduce(x, axis, n):
    k = 1
    while k < n:
        x = x + lax.ppermute(x, axis, xor_perm(n, lambda j, k=k: j ^ k))
        k *= 2
    return x


def xor_reduce_scatter(x, axis, n):
    i = lax.axis_index(axis)
    k = n // 2
    while k >= 1:
        half = x.shape[1] // 2
        bit = (i // k) % 2
        keep = lax.dynamic_slice_in_dim(x, bit * half, half, 1)
        send = lax.dynamic_slice_in_dim(x, (1 - bit) * half, half, 1)
        x = keep + lax.ppermute(send, axis, xor_perm(n, lambda j, k=k: j ^ k))
        k //= 2
    return x


def xor_gather_stack(x, axis, n, size):
    i = lax.axis_index(axis)
    stack = x[None]
    k = 1
    while k < size:
        other = lax.ppermute(stack, axis, xor_perm(n, lambda j, k=k: j ^ k))
        low = (i // k) % 2 == 0
        stack = jnp.where(
            low,
            jnp.concatenate([stack, other], axis=0),
            jnp.concatenate([other, stack], axis=0),
        )
        k *= 2
    return stack


def power_of_two(n):
    return n & (n - 1) == 0


def gather_pieces(blk, n):
    i = lax.axis_index("seq")
    rows = blk.shape[0]
    if n != 8:
        full = lax.all_gather(blk, "seq", axis=0, tiled=True)
        return [(full, jnp.int32(0), n * rows)]
    core = i % 2
    chip = i // 2
    sib = lax.ppermute(blk, "seq", xor_perm(8, lambda j: j ^ 1))
    pair = jnp.concatenate([blk, sib], axis=0)
    nb = lax.ppermute(pair, "seq", xor_perm(8, lambda j: j ^ 2 if j % 2 == 0 else j ^ 4))
    dg = lax.ppermute(nb[:rows], "seq", xor_perm(8, lambda j: j ^ 5 if j % 2 == 0 else j ^ 3))
    oth = lax.ppermute(jnp.concatenate([nb, dg], axis=0), "seq", xor_perm(8, lambda j: j ^ 1))
    nb_chip = chip ^ (1 + core)
    oth_chip = chip ^ (2 - core)
    diag = chip ^ 3
    return [
        (blk, i, rows),
        (sib, i ^ 1, rows),
        (nb[:rows], 2 * nb_chip + core, rows),
        (nb[rows:], 2 * nb_chip + 1 - core, rows),
        (dg, 2 * diag + 1 - core, rows),
        (oth[:rows], 2 * oth_chip + 1 - core, rows),
        (oth[rows : 2 * rows], 2 * oth_chip + core, rows),
        (oth[2 * rows :], 2 * diag + core, rows),
    ]


def project(normed, pieces):
    total = None
    for piece, source, rows in pieces:
        cols = lax.dynamic_slice_in_dim(normed, source * rows, rows, 1)
        term = jnp.dot(cols, piece, preferred_element_type=jnp.float32)
        total = term if total is None else total + term
    return total


def shards(
    hidden, norm_gain, w_query, w_key, w_value, doc_lengths, critic_up, critic_down, rule_ids
):
    n_seq = lax.axis_size("seq")
    n_tp = lax.axis_size("tp")
    seq_i = lax.axis_index("seq")
    tp_i = lax.axis_index("tp")
    normed = rms_norm(hidden, norm_gain)
    tokens_here = hidden.shape[0]
    d_rows = w_query.shape[0]
    heads_here = w_query.shape[1] // HEAD
    sharers = GROUP // heads_here
    kv_width = HEAD // sharers
    kv_head = tp_i * heads_here // GROUP
    kv_part = tp_i % sharers
    kv_start = kv_head * HEAD + kv_part * kv_width
    key_cols = lax.dynamic_slice_in_dim(w_key, kv_start, kv_width, 1)
    value_cols = lax.dynamic_slice_in_dim(w_value, kv_start, kv_width, 1)
    kv_weights = jnp.concatenate([key_cols, value_cols], axis=1)

    doc_ends = jnp.cumsum(doc_lengths) - 1
    first_row = seq_i * tokens_here
    query_pos = first_row + jnp.arange(tokens_here, dtype=jnp.int32)
    picker = (doc_ends[:, None] == query_pos[None, :]).astype(jnp.bfloat16)
    end_terms = jnp.dot(picker, normed, preferred_element_type=jnp.float32).astype(jnp.bfloat16)
    if power_of_two(n_seq):
        end_rows = xor_reduce_scatter(end_terms, "seq", n_seq)
    else:
        end_rows = lax.psum_scatter(end_terms, "seq", scatter_dimension=1, tiled=True)
    up_own = jnp.dot(end_rows, critic_up, preferred_element_type=jnp.float32)
    if power_of_two(n_seq):
        up_sum = xor_all_reduce(up_own, "seq", n_seq)
    else:
        up_sum = lax.psum(up_own, "seq")
    critic_hidden = jax.nn.silu(up_sum).astype(jnp.bfloat16)
    per_rule = jnp.einsum(
        "dc,rce->dre", critic_hidden, critic_down, preferred_element_type=jnp.float32
    )
    rule_pick = rule_ids[:, None] == jnp.arange(critic_down.shape[0], dtype=jnp.int32)[None, :]
    chosen = jnp.sum(jnp.where(rule_pick[:, :, None], per_rule, 0.0), axis=1)
    if power_of_two(n_tp):
        critic_sum = xor_all_reduce(chosen, "tp", n_tp)
    else:
        critic_sum = lax.psum(chosen, "tp")
    critic_values = critic_sum.astype(jnp.bfloat16)

    kv_pieces = gather_pieces(kv_weights, n_seq)
    kv_own = project(normed, kv_pieces).astype(jnp.bfloat16)
    kv_stack = xor_gather_stack(kv_own, "tp", n_tp, sharers)
    kv_rows = jnp.concatenate(
        [kv_stack[m, :, :kv_width] for m in range(sharers)]
        + [kv_stack[m, :, kv_width:] for m in range(sharers)],
        axis=1,
    )
    kv_all = gather_pieces(kv_rows, n_seq)
    key_block = jnp.concatenate([piece[:, :HEAD] for piece, _, _ in kv_all], axis=0)
    value_block = jnp.concatenate([piece[:, HEAD:] for piece, _, _ in kv_all], axis=0)
    key_pos = jnp.concatenate(
        [
            source * tokens_here + jnp.arange(piece.shape[0], dtype=jnp.int32)
            for piece, source, _ in kv_all
        ]
    )

    q_pieces = gather_pieces(w_query, n_seq)
    queries = project(normed, q_pieces).astype(jnp.bfloat16).reshape(tokens_here, heads_here, HEAD)

    def segment_of(positions):
        return jnp.sum((positions[:, None] > doc_ends[None, :]).astype(jnp.int32), axis=1)

    query_seg = segment_of(query_pos)
    inverse_root = 1.0 / math.sqrt(HEAD)
    allowed = (query_seg[:, None] == segment_of(key_pos)[None, :]) & (
        key_pos[None, :] <= query_pos[:, None]
    )
    allowed = allowed[:, None, :]
    scores = (
        jnp.einsum("qhd,kd->qhk", queries, key_block, preferred_element_type=jnp.float32)
        * inverse_root
    )
    scores = jnp.where(allowed, scores, -1e30)
    maxima = jnp.max(scores, axis=2)
    expanded = jnp.where(allowed, jnp.exp(scores - maxima[:, :, None]), 0.0)
    totals = jnp.sum(expanded, axis=2)
    weighted = jnp.einsum(
        "qhk,kd->qhd",
        expanded.astype(jnp.bfloat16),
        value_block,
        preferred_element_type=jnp.float32,
    )
    attention = (
        (weighted / totals[:, :, None])
        .reshape(tokens_here, heads_here * HEAD)
        .astype(jnp.bfloat16)
    )
    return (attention, critic_values)


def solution(mesh):
    return jax.shard_map(
        shards,
        mesh=mesh,
        in_specs=(
            P("seq", None),
            P(),
            P("seq", "tp"),
            P("seq", None),
            P("seq", None),
            P(),
            P("seq", "tp"),
            P(None, "tp", "seq"),
            P(),
        ),
        out_specs=(P("seq", "tp"), P(None, "seq")),
        check_vma=False,
    )
```

```python
import math

import jax
import jax.numpy as jnp
from jax import lax
from jax.sharding import PartitionSpec as P


HEAD = 128
GROUP = 8


def rms_norm(values, norm_gain):
    widened = values.astype(jnp.float32)
    mean_square = jnp.mean(widened * widened, axis=-1, keepdims=True)
    return (widened * lax.rsqrt(mean_square + 1e-05) * norm_gain.astype(jnp.float32)).astype(
        jnp.bfloat16
    )


def xor_perm(n, pick):
    return [(j, pick(j)) for j in range(n)]


def xor_all_reduce(x, axis, n):
    k = 1
    while k < n:
        x = x + lax.ppermute(x, axis, xor_perm(n, lambda j, k=k: j ^ k))
        k = k * 2
    return x


def xor_reduce_scatter(x, axis, n):
    i = lax.axis_index(axis)
    k = n // 2
    while k >= 1:
        half = x.shape[1] // 2
        bit = (i // k) % 2
        keep = lax.dynamic_slice_in_dim(x, bit * half, half, 1)
        send = lax.dynamic_slice_in_dim(x, (1 - bit) * half, half, 1)
        x = keep + lax.ppermute(send, axis, xor_perm(n, lambda j, k=k: j ^ k))
        k = k // 2
    return x


def xor_gather_stack(x, axis, n, size):
    i = lax.axis_index(axis)
    stack = x[None]
    k = 1
    while k < size:
        other = lax.ppermute(stack, axis, xor_perm(n, lambda j, k=k: j ^ k))
        low = (i // k) % 2 == 0
        stack = jnp.where(
            low,
            jnp.concatenate([stack, other], axis=0),
            jnp.concatenate([other, stack], axis=0),
        )
        k = k * 2
    return stack


def power_of_two(n):
    return n & (n - 1) == 0


def gather_pieces(blk, n):
    i = lax.axis_index("seq")
    rows = blk.shape[0]
    if n != 8:
        full = lax.all_gather(blk, "seq", axis=0, tiled=True)
        return [(full, jnp.int32(0), n * rows)]
    core = i % 2
    chip = i // 2
    sib = lax.ppermute(blk, "seq", xor_perm(8, lambda j: j ^ 1))
    pair = jnp.concatenate([blk, sib], axis=0)
    nb = lax.ppermute(pair, "seq", xor_perm(8, lambda j: j ^ 2 if j % 2 == 0 else j ^ 4))
    dg = lax.ppermute(nb[:rows], "seq", xor_perm(8, lambda j: j ^ 5 if j % 2 == 0 else j ^ 3))
    oth = lax.ppermute(jnp.concatenate([nb, dg], axis=0), "seq", xor_perm(8, lambda j: j ^ 1))
    nb_chip = chip ^ (1 + core)
    oth_chip = chip ^ (2 - core)
    diag = chip ^ 3
    return [
        (blk, i, rows),
        (sib, i ^ 1, rows),
        (nb[:rows], 2 * nb_chip + core, rows),
        (nb[rows:], 2 * nb_chip + 1 - core, rows),
        (dg, 2 * diag + 1 - core, rows),
        (oth[:rows], 2 * oth_chip + 1 - core, rows),
        (oth[rows : 2 * rows], 2 * oth_chip + core, rows),
        (oth[2 * rows :], 2 * diag + core, rows),
    ]


def project(normed, pieces):
    total = None
    for piece, source, rows in pieces:
        cols = lax.dynamic_slice_in_dim(normed, source * rows, rows, 1)
        term = jnp.dot(cols, piece, preferred_element_type=jnp.float32)
        total = term if total is None else total + term
    return total


def body(
    hidden, norm_gain, w_query, w_key, w_value, doc_lengths, critic_up, critic_down, rule_ids
):
    n_seq = lax.axis_size("seq")
    n_tp = lax.axis_size("tp")
    seq_i = lax.axis_index("seq")
    tp_i = lax.axis_index("tp")
    normed = rms_norm(hidden, norm_gain)
    tokens_here = hidden.shape[0]
    heads_here = w_query.shape[1] // HEAD
    sharers = GROUP // heads_here
    kv_width = HEAD // sharers
    kv_head = tp_i * heads_here // GROUP
    kv_part = tp_i % sharers
    kv_start = kv_head * HEAD + kv_part * kv_width
    key_cols = lax.dynamic_slice_in_dim(w_key, kv_start, kv_width, 1)
    value_cols = lax.dynamic_slice_in_dim(w_value, kv_start, kv_width, 1)
    kv_weights = jnp.concatenate([key_cols, value_cols], axis=1)

    doc_ends = jnp.cumsum(doc_lengths) - 1
    first_row = seq_i * tokens_here
    query_pos = first_row + jnp.arange(tokens_here, dtype=jnp.int32)
    picker = (doc_ends[:, None] == query_pos[None, :]).astype(jnp.bfloat16)
    end_terms = jnp.dot(picker, normed, preferred_element_type=jnp.float32).astype(jnp.bfloat16)
    if power_of_two(n_seq):
        end_rows = xor_reduce_scatter(end_terms, "seq", n_seq)
    else:
        end_rows = lax.psum_scatter(end_terms, "seq", scatter_dimension=1, tiled=True)
    up_own = jnp.dot(end_rows, critic_up, preferred_element_type=jnp.float32)
    if power_of_two(n_seq):
        up_sum = xor_all_reduce(up_own, "seq", n_seq)
    else:
        up_sum = lax.psum(up_own, "seq")
    critic_hidden = jax.nn.silu(up_sum).astype(jnp.bfloat16)
    per_rule = jnp.einsum(
        "dc,rce->dre", critic_hidden, critic_down, preferred_element_type=jnp.float32
    )
    rule_pick = rule_ids[:, None] == jnp.arange(critic_down.shape[0], dtype=jnp.int32)[None, :]
    chosen = jnp.sum(jnp.where(rule_pick[:, :, None], per_rule, 0.0), axis=1)
    if power_of_two(n_tp):
        critic_sum = xor_all_reduce(chosen, "tp", n_tp)
    else:
        critic_sum = lax.psum(chosen, "tp")
    critic_values = critic_sum.astype(jnp.bfloat16)

    kv_pieces = gather_pieces(kv_weights, n_seq)
    kv_own = project(normed, kv_pieces).astype(jnp.bfloat16)
    kv_stack = xor_gather_stack(kv_own, "tp", n_tp, sharers)
    kv_rows = jnp.concatenate(
        [kv_stack[m, :, :kv_width] for m in range(sharers)]
        + [kv_stack[m, :, kv_width:] for m in range(sharers)],
        axis=1,
    )
    kv_all = gather_pieces(kv_rows, n_seq)
    key_block = jnp.concatenate([piece[:, :HEAD] for piece, _, _ in kv_all], axis=0)
    value_block = jnp.concatenate([piece[:, HEAD:] for piece, _, _ in kv_all], axis=0)
    key_pos = jnp.concatenate(
        [
            source * tokens_here + jnp.arange(piece.shape[0], dtype=jnp.int32)
            for piece, source, _ in kv_all
        ]
    )

    q_pieces = gather_pieces(w_query, n_seq)
    queries = project(normed, q_pieces).astype(jnp.bfloat16).reshape(tokens_here, heads_here, HEAD)

    def segment_of(positions):
        return jnp.sum((positions[:, None] > doc_ends[None, :]).astype(jnp.int32), axis=1)

    query_seg = segment_of(query_pos)
    inverse_root = 1.0 / math.sqrt(HEAD)
    allowed = (query_seg[:, None] == segment_of(key_pos)[None, :]) & (
        key_pos[None, :] <= query_pos[:, None]
    )
    allowed = allowed[:, None, :]
    scores = (
        jnp.einsum("qhd,kd->qhk", queries, key_block, preferred_element_type=jnp.float32)
        * inverse_root
    )
    scores = jnp.where(allowed, scores, -1e30)
    maxima = jnp.max(scores, axis=2)
    expanded = jnp.where(allowed, jnp.exp(scores - maxima[:, :, None]), 0.0)
    totals = jnp.sum(expanded, axis=2)
    weighted = jnp.einsum(
        "qhk,kd->qhd",
        expanded.astype(jnp.bfloat16),
        value_block,
        preferred_element_type=jnp.float32,
    )
    attention = (
        (weighted / totals[:, :, None])
        .reshape(tokens_here, heads_here * HEAD)
        .astype(jnp.bfloat16)
    )
    return (attention, critic_values)


def solution(mesh):
    return jax.shard_map(
        body,
        mesh=mesh,
        in_specs=(
            P("seq", None),
            P(),
            P("seq", "tp"),
            P("seq", None),
            P("seq", None),
            P(),
            P("seq", "tp"),
            P(None, "tp", "seq"),
            P(),
        ),
        out_specs=(P("seq", "tp"), P(None, "seq")),
        check_vma=False,
    )
```

```python
import math

import jax
import jax.numpy as jnp
from jax import lax
from jax.sharding import PartitionSpec as P


HEAD = 128
GROUP = 8


def rms_norm(values, norm_gain):
    widened = values.astype(jnp.float32)
    mean_square = jnp.mean(widened * widened, axis=-1, keepdims=True)
    return (widened * lax.rsqrt(mean_square + 1e-05) * norm_gain.astype(jnp.float32)).astype(
        jnp.bfloat16
    )


def xor_perm(n, pick):
    return [(j, pick(j)) for j in range(n)]


def xor_all_reduce(x, axis, n):
    k = 1
    while k < n:
        x = x + lax.ppermute(x, axis, xor_perm(n, lambda j, k=k: j ^ k))
        k = k * 2
    return x


def xor_reduce_scatter(x, axis, n):
    i = lax.axis_index(axis)
    k = n // 2
    while k >= 1:
        half = x.shape[1] // 2
        bit = (i // k) % 2
        keep = lax.dynamic_slice_in_dim(x, bit * half, half, 1)
        send = lax.dynamic_slice_in_dim(x, (1 - bit) * half, half, 1)
        x = keep + lax.ppermute(send, axis, xor_perm(n, lambda j, k=k: j ^ k))
        k = k // 2
    return x


def xor_gather_stack(x, axis, n, size):
    i = lax.axis_index(axis)
    stack = x[None]
    k = 1
    while k < size:
        other = lax.ppermute(stack, axis, xor_perm(n, lambda j, k=k: j ^ k))
        low = (i // k) % 2 == 0
        stack = jnp.where(
            low,
            jnp.concatenate([stack, other], axis=0),
            jnp.concatenate([other, stack], axis=0),
        )
        k = k * 2
    return stack


def power_of_two(n):
    return n & (n - 1) == 0


def gather_pieces(blk, n):
    i = lax.axis_index("seq")
    if n != 8:
        full = lax.all_gather(blk, "seq", axis=0, tiled=False)
        return [(full[m], m) for m in range(n)]
    core = i % 2
    chip = i // 2
    sib = lax.ppermute(blk, "seq", xor_perm(8, lambda j: j ^ 1))
    rows = blk.shape[0]
    nb = lax.ppermute(
        jnp.concatenate([blk, sib], axis=0),
        "seq",
        xor_perm(8, lambda j: j ^ 2 if j % 2 == 0 else j ^ 4),
    )
    nb0, nb1 = nb[:rows], nb[rows:]
    dg = lax.ppermute(nb0, "seq", xor_perm(8, lambda j: j ^ 5 if j % 2 == 0 else j ^ 3))
    ot = lax.ppermute(jnp.concatenate([nb, dg], axis=0), "seq", xor_perm(8, lambda j: j ^ 1))
    ot0, ot1, ot2 = ot[:rows], ot[rows : 2 * rows], ot[2 * rows :]
    nb_chip = chip ^ (1 + core)
    oth_chip = chip ^ (2 - core)
    diag = chip ^ 3
    return [
        (blk, i),
        (sib, i ^ 1),
        (nb0, 2 * nb_chip + core),
        (nb1, 2 * nb_chip + 1 - core),
        (dg, 2 * diag + 1 - core),
        (ot0, 2 * oth_chip + 1 - core),
        (ot1, 2 * oth_chip + core),
        (ot2, 2 * diag + core),
    ]


def project(normed_split, pieces):
    total = None
    for piece, source in pieces:
        cols = lax.dynamic_index_in_dim(normed_split, source, 0, keepdims=False)
        term = jnp.dot(cols, piece, preferred_element_type=jnp.float32)
        total = term if total is None else total + term
    return total


def body(
    hidden, norm_gain, w_query, w_key, w_value, doc_lengths, critic_up, critic_down, rule_ids
):
    n_seq = lax.axis_size("seq")
    n_tp = lax.axis_size("tp")
    seq_i = lax.axis_index("seq")
    tp_i = lax.axis_index("tp")
    normed = rms_norm(hidden, norm_gain)
    tokens_here = hidden.shape[0]
    d_rows = w_query.shape[0]
    heads_here = w_query.shape[1] // HEAD
    sharers = GROUP // heads_here
    kv_width = HEAD // sharers
    kv_head = tp_i * heads_here // GROUP
    kv_part = tp_i % sharers
    kv_start = kv_head * HEAD + kv_part * kv_width
    key_cols = lax.dynamic_slice_in_dim(w_key, kv_start, kv_width, 1)
    value_cols = lax.dynamic_slice_in_dim(w_value, kv_start, kv_width, 1)
    weights = jnp.concatenate([w_query, key_cols, value_cols], axis=1)
    q_width = w_query.shape[1]
    normed_split = normed.reshape(tokens_here, n_seq, d_rows).transpose(1, 0, 2)

    doc_ends = jnp.cumsum(doc_lengths) - 1
    first_row = seq_i * tokens_here
    query_pos = first_row + jnp.arange(tokens_here, dtype=jnp.int32)
    picker = (doc_ends[:, None] == query_pos[None, :]).astype(jnp.bfloat16)
    end_terms = jnp.dot(picker, normed, preferred_element_type=jnp.float32).astype(jnp.bfloat16)
    if power_of_two(n_seq):
        end_rows = xor_reduce_scatter(end_terms, "seq", n_seq)
    else:
        end_rows = lax.psum_scatter(end_terms, "seq", scatter_dimension=1, tiled=True)
    up_own = jnp.dot(end_rows, critic_up, preferred_element_type=jnp.float32)
    if power_of_two(n_seq):
        up_sum = xor_all_reduce(up_own, "seq", n_seq)
    else:
        up_sum = lax.psum(up_own, "seq")
    critic_hidden = jax.nn.silu(up_sum).astype(jnp.bfloat16)
    per_rule = jnp.einsum(
        "dc,rce->dre", critic_hidden, critic_down, preferred_element_type=jnp.float32
    )
    rule_pick = rule_ids[:, None] == jnp.arange(critic_down.shape[0], dtype=jnp.int32)[None, :]
    chosen = jnp.sum(jnp.where(rule_pick[:, :, None], per_rule, 0.0), axis=1)
    if power_of_two(n_tp):
        critic_sum = xor_all_reduce(chosen, "tp", n_tp)
    else:
        critic_sum = lax.psum(chosen, "tp")
    critic_values = critic_sum.astype(jnp.bfloat16)

    projected = project(normed_split, gather_pieces(weights, n_seq))
    kv_own = projected[:, q_width:].astype(jnp.bfloat16)
    kv_stack = xor_gather_stack(kv_own, "tp", n_tp, sharers)
    kv_rows = jnp.concatenate(
        [kv_stack[m, :, :kv_width] for m in range(sharers)]
        + [kv_stack[m, :, kv_width:] for m in range(sharers)],
        axis=1,
    )
    kv_all = gather_pieces(kv_rows, n_seq)
    key_block = jnp.concatenate([piece[:, :HEAD] for piece, _ in kv_all], axis=0)
    value_block = jnp.concatenate([piece[:, HEAD:] for piece, _ in kv_all], axis=0)
    key_pos = jnp.concatenate(
        [
            source * tokens_here + jnp.arange(piece.shape[0], dtype=jnp.int32)
            for piece, source in kv_all
        ]
    )

    queries = (
        projected[:, :q_width].astype(jnp.bfloat16).reshape(tokens_here, heads_here, HEAD)
    )

    def segment_of(positions):
        return jnp.sum((positions[:, None] > doc_ends[None, :]).astype(jnp.int32), axis=1)

    query_seg = segment_of(query_pos)
    inverse_root = 1.0 / math.sqrt(HEAD)
    allowed = (query_seg[:, None] == segment_of(key_pos)[None, :]) & (
        key_pos[None, :] <= query_pos[:, None]
    )
    allowed = allowed[:, None, :]
    scores = (
        jnp.einsum("qhd,kd->qhk", queries, key_block, preferred_element_type=jnp.float32)
        * inverse_root
    )
    scores = jnp.where(allowed, scores, -1e30)
    maxima = jnp.max(scores, axis=2)
    expanded = jnp.where(allowed, jnp.exp(scores - maxima[:, :, None]), 0.0)
    totals = jnp.sum(expanded, axis=2)
    weighted = jnp.einsum(
        "qhk,kd->qhd",
        expanded.astype(jnp.bfloat16),
        value_block,
        preferred_element_type=jnp.float32,
    )
    attention = (
        (weighted / totals[:, :, None])
        .reshape(tokens_here, heads_here * HEAD)
        .astype(jnp.bfloat16)
    )
    return (attention, critic_values)


def solution(mesh):
    return jax.shard_map(
        body,
        mesh=mesh,
        in_specs=(
            P("seq", None),
            P(),
            P("seq", "tp"),
            P("seq", None),
            P("seq", None),
            P(),
            P("seq", "tp"),
            P(None, "tp", "seq"),
            P(),
        ),
        out_specs=(P("seq", "tp"), P(None, "seq")),
        check_vma=False,
    )
```

```python
import math

import jax
import jax.numpy as jnp
from jax import lax
from jax.sharding import PartitionSpec as P


HEAD = 128
GROUP = 8


def rms_norm(values, norm_gain):
    widened = values.astype(jnp.float32)
    mean_square = jnp.mean(widened * widened, axis=-1, keepdims=True)
    return (widened * lax.rsqrt(mean_square + 1e-05) * norm_gain.astype(jnp.float32)).astype(
        jnp.bfloat16
    )


def xor_perm(n, pick):
    return [(j, pick(j)) for j in range(n)]


def xor_all_reduce(x, axis, n):
    k = 1
    while k < n:
        x = x + lax.ppermute(x, axis, xor_perm(n, lambda j, k=k: j ^ k))
        k = k * 2
    return x


def xor_reduce_scatter(x, axis, n):
    i = lax.axis_index(axis)
    k = n // 2
    while k >= 1:
        half = x.shape[1] // 2
        bit = (i // k) % 2
        keep = lax.dynamic_slice_in_dim(x, bit * half, half, 1)
        send = lax.dynamic_slice_in_dim(x, (1 - bit) * half, half, 1)
        x = keep + lax.ppermute(send, axis, xor_perm(n, lambda j, k=k: j ^ k))
        k = k // 2
    return x


def xor_gather_stack(x, axis, n, size):
    i = lax.axis_index(axis)
    stack = x[None]
    k = 1
    while k < size:
        other = lax.ppermute(stack, axis, xor_perm(n, lambda j, k=k: j ^ k))
        low = (i // k) % 2 == 0
        stack = jnp.where(
            low,
            jnp.concatenate([stack, other], axis=0),
            jnp.concatenate([other, stack], axis=0),
        )
        k = k * 2
    return stack


def power_of_two(n):
    return n & (n - 1) == 0


def gather_pieces(blk, n):
    i = lax.axis_index("seq")
    rows = blk.shape[0]
    if n != 8:
        full = lax.all_gather(blk, "seq", axis=0, tiled=True)
        return [(full, jnp.int32(0), n * rows)]
    core = i % 2
    chip = i // 2
    sib = lax.ppermute(blk, "seq", xor_perm(8, lambda j: j ^ 1))
    pair = jnp.concatenate([blk, sib], axis=0)
    nb = lax.ppermute(pair, "seq", xor_perm(8, lambda j: j ^ 2 if j % 2 == 0 else j ^ 4))
    dg = lax.ppermute(nb[:rows], "seq", xor_perm(8, lambda j: j ^ 5 if j % 2 == 0 else j ^ 3))
    oth = lax.ppermute(jnp.concatenate([nb, dg], axis=0), "seq", xor_perm(8, lambda j: j ^ 1))
    nb_chip = chip ^ (1 + core)
    oth_chip = chip ^ (2 - core)
    diag = chip ^ 3
    return [
        (blk, i, rows),
        (sib, i ^ 1, rows),
        (nb[:rows], 2 * nb_chip + core, rows),
        (nb[rows:], 2 * nb_chip + 1 - core, rows),
        (dg, 2 * diag + 1 - core, rows),
        (oth[:rows], 2 * oth_chip + 1 - core, rows),
        (oth[rows : 2 * rows], 2 * oth_chip + core, rows),
        (oth[2 * rows :], 2 * diag + core, rows),
    ]


def project(normed, pieces):
    total = None
    for piece, source, rows in pieces:
        cols = lax.dynamic_slice_in_dim(normed, source * rows, rows, 1)
        term = jnp.dot(cols, piece, preferred_element_type=jnp.float32)
        total = term if total is None else total + term
    return total


def body(
    hidden, norm_gain, w_query, w_key, w_value, doc_lengths, critic_up, critic_down, rule_ids
):
    n_seq = lax.axis_size("seq")
    n_tp = lax.axis_size("tp")
    seq_i = lax.axis_index("seq")
    tp_i = lax.axis_index("tp")
    normed = rms_norm(hidden, norm_gain)
    tokens_here = hidden.shape[0]
    heads_here = w_query.shape[1] // HEAD
    sharers = GROUP // heads_here
    kv_width = HEAD // sharers
    kv_head = tp_i * heads_here // GROUP
    kv_part = tp_i % sharers
    kv_start = kv_head * HEAD + kv_part * kv_width
    key_cols = lax.dynamic_slice_in_dim(w_key, kv_start, kv_width, 1)
    value_cols = lax.dynamic_slice_in_dim(w_value, kv_start, kv_width, 1)
    kv_weights = jnp.concatenate([key_cols, value_cols], axis=1)

    doc_ends = jnp.cumsum(doc_lengths) - 1
    first_row = seq_i * tokens_here
    query_pos = first_row + jnp.arange(tokens_here, dtype=jnp.int32)
    picker = (doc_ends[:, None] == query_pos[None, :]).astype(jnp.bfloat16)
    end_terms = jnp.dot(picker, normed, preferred_element_type=jnp.float32).astype(jnp.bfloat16)
    if power_of_two(n_seq):
        end_rows = xor_reduce_scatter(end_terms, "seq", n_seq)
    else:
        end_rows = lax.psum_scatter(end_terms, "seq", scatter_dimension=1, tiled=True)
    up_own = jnp.dot(end_rows, critic_up, preferred_element_type=jnp.float32)
    if power_of_two(n_seq):
        up_sum = xor_all_reduce(up_own, "seq", n_seq)
    else:
        up_sum = lax.psum(up_own, "seq")
    critic_hidden = jax.nn.silu(up_sum).astype(jnp.bfloat16)
    per_rule = jnp.einsum(
        "dc,rce->dre", critic_hidden, critic_down, preferred_element_type=jnp.float32
    )
    rule_pick = rule_ids[:, None] == jnp.arange(critic_down.shape[0], dtype=jnp.int32)[None, :]
    chosen = jnp.sum(jnp.where(rule_pick[:, :, None], per_rule, 0.0), axis=1)
    if power_of_two(n_tp):
        critic_sum = xor_all_reduce(chosen, "tp", n_tp)
    else:
        critic_sum = lax.psum(chosen, "tp")
    critic_values = critic_sum.astype(jnp.bfloat16)

    kv_pieces = gather_pieces(kv_weights, n_seq)
    kv_own = project(normed, kv_pieces).astype(jnp.bfloat16)
    kv_stack = xor_gather_stack(kv_own, "tp", n_tp, sharers)
    kv_rows = jnp.concatenate(
        [kv_stack[m, :, :kv_width] for m in range(sharers)]
        + [kv_stack[m, :, kv_width:] for m in range(sharers)],
        axis=1,
    )
    kv_all = gather_pieces(kv_rows, n_seq)
    key_block = jnp.concatenate([piece[:, :HEAD] for piece, _, _ in kv_all], axis=0)
    value_block = jnp.concatenate([piece[:, HEAD:] for piece, _, _ in kv_all], axis=0)
    key_pos = jnp.concatenate(
        [
            source * tokens_here + jnp.arange(piece.shape[0], dtype=jnp.int32)
            for piece, source, _ in kv_all
        ]
    )

    q_weights = lax.all_gather(w_query, "seq", axis=0, tiled=True)
    queries = (
        jnp.dot(normed, q_weights, preferred_element_type=jnp.float32)
        .astype(jnp.bfloat16)
        .reshape(tokens_here, heads_here, HEAD)
    )

    def segment_of(positions):
        return jnp.sum((positions[:, None] > doc_ends[None, :]).astype(jnp.int32), axis=1)

    query_seg = segment_of(query_pos)
    inverse_root = 1.0 / math.sqrt(HEAD)
    allowed = (query_seg[:, None] == segment_of(key_pos)[None, :]) & (
        key_pos[None, :] <= query_pos[:, None]
    )
    allowed = allowed[:, None, :]
    scores = (
        jnp.einsum("qhd,kd->qhk", queries, key_block, preferred_element_type=jnp.float32)
        * inverse_root
    )
    scores = jnp.where(allowed, scores, -1e30)
    maxima = jnp.max(scores, axis=2)
    expanded = jnp.where(allowed, jnp.exp(scores - maxima[:, :, None]), 0.0)
    totals = jnp.sum(expanded, axis=2)
    weighted = jnp.einsum(
        "qhk,kd->qhd",
        expanded.astype(jnp.bfloat16),
        value_block,
        preferred_element_type=jnp.float32,
    )
    attention = (
        (weighted / totals[:, :, None])
        .reshape(tokens_here, heads_here * HEAD)
        .astype(jnp.bfloat16)
    )
    return (attention, critic_values)


def solution(mesh):
    return jax.shard_map(
        body,
        mesh=mesh,
        in_specs=(
            P("seq", None),
            P(),
            P("seq", "tp"),
            P("seq", None),
            P("seq", None),
            P(),
            P("seq", "tp"),
            P(None, "tp", "seq"),
            P(),
        ),
        out_specs=(P("seq", "tp"), P(None, "seq")),
        check_vma=False,
    )
```

```python
import math

import jax
import jax.numpy as jnp
from jax import lax
from jax.sharding import PartitionSpec as P


HEAD = 128
GROUP = 8


def rms_norm(values, norm_gain):
    widened = values.astype(jnp.float32)
    mean_square = jnp.mean(widened * widened, axis=-1, keepdims=True)
    return (widened * lax.rsqrt(mean_square + 1e-05) * norm_gain.astype(jnp.float32)).astype(
        jnp.bfloat16
    )


def xor_perm(n, pick):
    return [(j, pick(j)) for j in range(n)]


def xor_all_reduce(x, axis, n):
    k = 1
    while k < n:
        x = x + lax.ppermute(x, axis, xor_perm(n, lambda j, k=k: j ^ k))
        k = k * 2
    return x


def xor_reduce_scatter(x, axis, n):
    i = lax.axis_index(axis)
    k = n // 2
    while k >= 1:
        half = x.shape[1] // 2
        bit = (i // k) % 2
        keep = lax.dynamic_slice_in_dim(x, bit * half, half, 1)
        send = lax.dynamic_slice_in_dim(x, (1 - bit) * half, half, 1)
        x = keep + lax.ppermute(send, axis, xor_perm(n, lambda j, k=k: j ^ k))
        k = k // 2
    return x


def power_of_two(n):
    return n & (n - 1) == 0


def gather_pieces(blk, n):
    i = lax.axis_index("seq")
    rows = blk.shape[0]
    if n != 8:
        full = lax.all_gather(blk, "seq", axis=0, tiled=False)
        return [(full[m], m, rows) for m in range(n)]
    core = i % 2
    chip = i // 2
    sib = lax.ppermute(blk, "seq", xor_perm(8, lambda j: j ^ 1))
    pair = jnp.concatenate([blk, sib], axis=0)
    nb = lax.ppermute(pair, "seq", xor_perm(8, lambda j: j ^ 2 if j % 2 == 0 else j ^ 4))
    dg = lax.ppermute(nb[:rows], "seq", xor_perm(8, lambda j: j ^ 5 if j % 2 == 0 else j ^ 3))
    oth = lax.ppermute(jnp.concatenate([nb, dg], axis=0), "seq", xor_perm(8, lambda j: j ^ 1))
    nb_chip = chip ^ (1 + core)
    oth_chip = chip ^ (2 - core)
    diag = chip ^ 3
    return [
        (blk, i, rows),
        (sib, i ^ 1, rows),
        (nb[:rows], 2 * nb_chip + core, rows),
        (nb[rows:], 2 * nb_chip + 1 - core, rows),
        (dg, 2 * diag + 1 - core, rows),
        (oth[:rows], 2 * oth_chip + 1 - core, rows),
        (oth[rows : 2 * rows], 2 * oth_chip + core, rows),
        (oth[2 * rows :], 2 * diag + core, rows),
    ]


def project(normed, pieces, stride, offset=0):
    total = None
    for piece, source, rows in pieces:
        cols = lax.dynamic_slice_in_dim(normed, source * stride + offset, rows, 1)
        term = jnp.dot(cols, piece, preferred_element_type=jnp.float32)
        total = term if total is None else total + term
    return total


def body(
    hidden, norm_gain, w_query, w_key, w_value, doc_lengths, critic_up, critic_down, rule_ids
):
    n_seq = lax.axis_size("seq")
    n_tp = lax.axis_size("tp")
    seq_i = lax.axis_index("seq")
    tp_i = lax.axis_index("tp")
    normed = rms_norm(hidden, norm_gain)
    tokens_here = hidden.shape[0]
    d_rows = w_query.shape[0]
    heads_here = w_query.shape[1] // HEAD
    sharers = GROUP // heads_here
    kv_rows_here = d_rows // sharers
    kv_head = tp_i * heads_here // GROUP
    kv_part = tp_i % sharers
    kv_weights = jnp.concatenate(
        [
            lax.dynamic_slice(w_key, (kv_part * kv_rows_here, kv_head * HEAD), (kv_rows_here, HEAD)),
            lax.dynamic_slice(w_value, (kv_part * kv_rows_here, kv_head * HEAD), (kv_rows_here, HEAD)),
        ],
        axis=1,
    )

    doc_ends = jnp.cumsum(doc_lengths) - 1
    first_row = seq_i * tokens_here
    query_pos = first_row + jnp.arange(tokens_here, dtype=jnp.int32)
    picker = (doc_ends[:, None] == query_pos[None, :]).astype(jnp.bfloat16)
    end_terms = jnp.dot(picker, normed, preferred_element_type=jnp.float32).astype(jnp.bfloat16)
    if power_of_two(n_seq):
        end_rows = xor_reduce_scatter(end_terms, "seq", n_seq)
    else:
        end_rows = lax.psum_scatter(end_terms, "seq", scatter_dimension=1, tiled=True)
    up_own = jnp.dot(end_rows, critic_up, preferred_element_type=jnp.float32)
    if power_of_two(n_seq):
        up_sum = xor_all_reduce(up_own, "seq", n_seq)
    else:
        up_sum = lax.psum(up_own, "seq")
    critic_hidden = jax.nn.silu(up_sum).astype(jnp.bfloat16)
    per_rule = jnp.einsum(
        "dc,rce->dre", critic_hidden, critic_down, preferred_element_type=jnp.float32
    )
    rule_pick = rule_ids[:, None] == jnp.arange(critic_down.shape[0], dtype=jnp.int32)[None, :]
    chosen = jnp.sum(jnp.where(rule_pick[:, :, None], per_rule, 0.0), axis=1)
    if power_of_two(n_tp):
        critic_sum = xor_all_reduce(chosen, "tp", n_tp)
    else:
        critic_sum = lax.psum(chosen, "tp")
    critic_values = critic_sum.astype(jnp.bfloat16)

    kv_pieces = gather_pieces(kv_weights, n_seq)
    kv_part_sum = project(normed, kv_pieces, d_rows, kv_part * kv_rows_here)
    kv_rows = kv_part_sum
    k = 1
    while k < sharers:
        kv_rows = kv_rows + lax.ppermute(kv_rows, "tp", xor_perm(n_tp, lambda j, k=k: j ^ k))
        k *= 2
    kv_rows = kv_rows.astype(jnp.bfloat16)
    kv_all = gather_pieces(kv_rows, n_seq)
    key_block = jnp.concatenate([piece[:, :HEAD] for piece, _, _ in kv_all], axis=0)
    value_block = jnp.concatenate([piece[:, HEAD:] for piece, _, _ in kv_all], axis=0)
    key_pos = jnp.concatenate(
        [
            source * tokens_here + jnp.arange(piece.shape[0], dtype=jnp.int32)
            for piece, source, _ in kv_all
        ]
    )

    q_weights = lax.all_gather(w_query, "seq", axis=0, tiled=True)
    queries = (
        jnp.dot(normed, q_weights, preferred_element_type=jnp.float32)
        .astype(jnp.bfloat16)
        .reshape(tokens_here, heads_here, HEAD)
    )

    def segment_of(positions):
        return jnp.sum((positions[:, None] > doc_ends[None, :]).astype(jnp.int32), axis=1)

    query_seg = segment_of(query_pos)
    inverse_root = 1.0 / math.sqrt(HEAD)
    allowed = (query_seg[:, None] == segment_of(key_pos)[None, :]) & (
        key_pos[None, :] <= query_pos[:, None]
    )
    outs = []
    for h in range(heads_here):
        scores = (
            jnp.dot(queries[:, h, :], key_block.T, preferred_element_type=jnp.float32)
            * inverse_root
        )
        scores = jnp.where(allowed, scores, -1e30)
        maxima = jnp.max(scores, axis=1, keepdims=True)
        expanded = jnp.where(allowed, jnp.exp(scores - maxima), 0.0)
        totals = jnp.sum(expanded, axis=1, keepdims=True)
        weighted = jnp.dot(
            expanded.astype(jnp.bfloat16), value_block, preferred_element_type=jnp.float32
        )
        outs.append((weighted / totals).astype(jnp.bfloat16))
    attention = jnp.concatenate(outs, axis=1)
    return (attention, critic_values)


def solution(mesh):
    return jax.shard_map(
        body,
        mesh=mesh,
        in_specs=(
            P("seq", None),
            P(),
            P("seq", "tp"),
            P("seq", None),
            P("seq", None),
            P(),
            P("seq", "tp"),
            P(None, "tp", "seq"),
            P(),
        ),
        out_specs=(P("seq", "tp"), P(None, "seq")),
        check_vma=False,
    )
```

```python
import math

import jax
import jax.numpy as jnp
from jax import lax
from jax.sharding import PartitionSpec as P


HEAD = 128
GROUP = 8


def rms_norm(values, norm_gain):
    widened = values.astype(jnp.float32)
    mean_square = jnp.mean(widened * widened, axis=-1, keepdims=True)
    return (widened * lax.rsqrt(mean_square + 1e-05) * norm_gain.astype(jnp.float32)).astype(
        jnp.bfloat16
    )


def xor_perm(n, pick):
    return [(j, pick(j)) for j in range(n)]


def seq_all_reduce(x):
    x = x + lax.ppermute(x, "seq", xor_perm(8, lambda j: j ^ 1))
    got = [lax.ppermute(x, "seq", xor_perm(8, lambda j, m=m: j ^ m)) for m in (2, 4, 6)]
    return x + got[0] + got[1] + got[2]


def seq_reduce_scatter(x):
    i = lax.axis_index("seq")
    chip_cols = x.shape[1] // 4
    own = lax.dynamic_slice_in_dim(x, (i // 2) * chip_cols, chip_cols, 1).astype(jnp.float32)
    for m in (2, 4, 6):
        part = lax.dynamic_slice_in_dim(x, ((i ^ m) // 2) * chip_cols, chip_cols, 1)
        own = own + lax.ppermute(part, "seq", xor_perm(8, lambda j, m=m: j ^ m)).astype(jnp.float32)
    half = chip_cols // 2
    core = i % 2
    keep = lax.dynamic_slice_in_dim(own, core * half, half, 1)
    send = lax.dynamic_slice_in_dim(own, (1 - core) * half, half, 1)
    return keep + lax.ppermute(send, "seq", xor_perm(8, lambda j: j ^ 1))


def group_sum(x, axis, n, size, canonical):
    got = [x] + [lax.ppermute(x, axis, xor_perm(n, lambda j, k=k: j ^ k)) for k in range(1, size)]
    if not canonical:
        total = got[0]
        for g in got[1:]:
            total = total + g
        return total
    me = lax.axis_index(axis) % size
    total = None
    for m in range(size):
        value = got[0]
        for k in range(1, size):
            value = jnp.where((me ^ k) == m, got[k], value)
        total = value if total is None else total + value
    return total


def power_of_two(n):
    return n & (n - 1) == 0


def gather_pieces(blk, n):
    i = lax.axis_index("seq")
    rows = blk.shape[0]
    if n != 8:
        full = lax.all_gather(blk, "seq", axis=0, tiled=False)
        return [(full[m], m, rows) for m in range(n)]
    sib = lax.ppermute(blk, "seq", xor_perm(8, lambda j: j ^ 1))
    pair = jnp.concatenate([blk, sib], axis=0)
    pieces = [(blk, i, rows), (sib, i ^ 1, rows)]
    for m in (2, 4, 6):
        got = lax.ppermute(pair, "seq", xor_perm(8, lambda j, m=m: j ^ m))
        pieces += [(got[:rows], i ^ m, rows), (got[rows:], i ^ m ^ 1, rows)]
    return pieces


def project(normed, pieces, stride, offset=0):
    total = None
    for piece, source, rows in pieces:
        cols = lax.dynamic_slice_in_dim(normed, source * stride + offset, rows, 1)
        term = jnp.dot(cols, piece, preferred_element_type=jnp.float32)
        total = term if total is None else total + term
    return total


def body(
    hidden, norm_gain, w_query, w_key, w_value, doc_lengths, critic_up, critic_down, rule_ids
):
    n_seq = lax.axis_size("seq")
    n_tp = lax.axis_size("tp")
    seq_i = lax.axis_index("seq")
    tp_i = lax.axis_index("tp")
    normed = rms_norm(hidden, norm_gain)
    tokens_here = hidden.shape[0]
    d_rows = w_query.shape[0]
    heads_here = w_query.shape[1] // HEAD
    sharers = GROUP // heads_here
    kv_rows_here = d_rows // sharers
    kv_head = tp_i * heads_here // GROUP
    kv_part = tp_i % sharers
    kv_weights = jnp.concatenate(
        [
            lax.dynamic_slice(w_key, (kv_part * kv_rows_here, kv_head * HEAD), (kv_rows_here, HEAD)),
            lax.dynamic_slice(w_value, (kv_part * kv_rows_here, kv_head * HEAD), (kv_rows_here, HEAD)),
        ],
        axis=1,
    )

    doc_ends = jnp.cumsum(doc_lengths) - 1
    first_row = seq_i * tokens_here
    query_pos = first_row + jnp.arange(tokens_here, dtype=jnp.int32)
    picker = (doc_ends[:, None] == query_pos[None, :]).astype(jnp.bfloat16)
    end_terms = jnp.dot(picker, normed, preferred_element_type=jnp.float32).astype(jnp.bfloat16)
    if n_seq == 8:
        end_rows = seq_reduce_scatter(end_terms).astype(jnp.bfloat16)
    else:
        end_rows = lax.psum_scatter(end_terms, "seq", scatter_dimension=1, tiled=True)
    up_own = jnp.dot(end_rows, critic_up, preferred_element_type=jnp.float32)
    if n_seq == 8:
        up_sum = seq_all_reduce(up_own)
    else:
        up_sum = lax.psum(up_own, "seq")
    critic_hidden = jax.nn.silu(up_sum).astype(jnp.bfloat16)
    per_rule = jnp.einsum(
        "dc,rce->dre", critic_hidden, critic_down, preferred_element_type=jnp.float32
    )
    rule_pick = rule_ids[:, None] == jnp.arange(critic_down.shape[0], dtype=jnp.int32)[None, :]
    chosen = jnp.sum(jnp.where(rule_pick[:, :, None], per_rule, 0.0), axis=1)
    if n_tp <= 8 and power_of_two(n_tp):
        critic_sum = group_sum(chosen, "tp", n_tp, n_tp, canonical=True)
    else:
        critic_sum = lax.psum(chosen, "tp")
    critic_values = critic_sum.astype(jnp.bfloat16)

    kv_pieces = gather_pieces(kv_weights, n_seq)
    kv_part_sum = project(normed, kv_pieces, d_rows, kv_part * kv_rows_here)
    kv_rows = group_sum(kv_part_sum, "tp", n_tp, sharers, canonical=False)
    kv_rows = kv_rows.astype(jnp.bfloat16)
    kv_all = gather_pieces(kv_rows, n_seq)
    key_block = jnp.concatenate([piece[:, :HEAD] for piece, _, _ in kv_all], axis=0)
    value_block = jnp.concatenate([piece[:, HEAD:] for piece, _, _ in kv_all], axis=0)
    key_pos = jnp.concatenate(
        [
            source * tokens_here + jnp.arange(piece.shape[0], dtype=jnp.int32)
            for piece, source, _ in kv_all
        ]
    )

    q_weights = lax.all_gather(w_query, "seq", axis=0, tiled=True)
    queries = (
        jnp.dot(normed, q_weights, preferred_element_type=jnp.float32)
        .astype(jnp.bfloat16)
        .reshape(tokens_here, heads_here, HEAD)
    )

    def segment_of(positions):
        return jnp.sum((positions[:, None] > doc_ends[None, :]).astype(jnp.int32), axis=1)

    query_seg = segment_of(query_pos)
    inverse_root = 1.0 / math.sqrt(HEAD)
    allowed = (query_seg[:, None] == segment_of(key_pos)[None, :]) & (
        key_pos[None, :] <= query_pos[:, None]
    )
    outs = []
    for h in range(heads_here):
        scores = (
            jnp.dot(queries[:, h, :], key_block.T, preferred_element_type=jnp.float32)
            * inverse_root
        )
        scores = jnp.where(allowed, scores, -1e30)
        maxima = jnp.max(scores, axis=1, keepdims=True)
        expanded = jnp.where(allowed, jnp.exp(scores - maxima), 0.0)
        totals = jnp.sum(expanded, axis=1, keepdims=True)
        weighted = jnp.dot(
            expanded.astype(jnp.bfloat16), value_block, preferred_element_type=jnp.float32
        )
        outs.append((weighted / totals).astype(jnp.bfloat16))
    attention = jnp.concatenate(outs, axis=1)
    return (attention, critic_values)


def solution(mesh):
    return jax.shard_map(
        body,
        mesh=mesh,
        in_specs=(
            P("seq", None),
            P(),
            P("seq", "tp"),
            P("seq", None),
            P("seq", None),
            P(),
            P("seq", "tp"),
            P(None, "tp", "seq"),
            P(),
        ),
        out_specs=(P("seq", "tp"), P(None, "seq")),
        check_vma=False,
    )
```

```python
import math

import jax
import jax.numpy as jnp
from jax import lax
from jax.sharding import PartitionSpec as P


HEAD = 128
GROUP = 8


def rms_norm(values, norm_gain):
    widened = values.astype(jnp.float32)
    mean_square = jnp.mean(widened * widened, axis=-1, keepdims=True)
    return (widened * lax.rsqrt(mean_square + 1e-05) * norm_gain.astype(jnp.float32)).astype(
        jnp.bfloat16
    )


def xor_perm(n, pick):
    return [(j, pick(j)) for j in range(n)]


def seq_all_reduce(x):
    x = x + lax.ppermute(x, "seq", xor_perm(8, lambda j: j ^ 1))
    got = [lax.ppermute(x, "seq", xor_perm(8, lambda j, m=m: j ^ m)) for m in (2, 4, 6)]
    return x + got[0] + got[1] + got[2]


def seq_reduce_scatter(x):
    i = lax.axis_index("seq")
    chip_cols = x.shape[1] // 4
    own = lax.dynamic_slice_in_dim(x, (i // 2) * chip_cols, chip_cols, 1).astype(jnp.float32)
    for m in (2, 4, 6):
        part = lax.dynamic_slice_in_dim(x, ((i ^ m) // 2) * chip_cols, chip_cols, 1)
        own = own + lax.ppermute(part, "seq", xor_perm(8, lambda j, m=m: j ^ m)).astype(jnp.float32)
    half = chip_cols // 2
    core = i % 2
    keep = lax.dynamic_slice_in_dim(own, core * half, half, 1)
    send = lax.dynamic_slice_in_dim(own, (1 - core) * half, half, 1)
    return keep + lax.ppermute(send, "seq", xor_perm(8, lambda j: j ^ 1))


def group_sum(x, axis, n, size, canonical):
    got = [x] + [lax.ppermute(x, axis, xor_perm(n, lambda j, k=k: j ^ k)) for k in range(1, size)]
    if not canonical:
        total = got[0]
        for g in got[1:]:
            total = total + g
        return total
    me = lax.axis_index(axis) % size
    total = None
    for m in range(size):
        value = got[0]
        for k in range(1, size):
            value = jnp.where((me ^ k) == m, got[k], value)
        total = value if total is None else total + value
    return total


def power_of_two(n):
    return n & (n - 1) == 0


def gather_pieces(blk, n):
    i = lax.axis_index("seq")
    rows = blk.shape[0]
    if n != 8:
        full = lax.all_gather(blk, "seq", axis=0, tiled=False)
        return [(full[m], m, rows) for m in range(n)]
    sib = lax.ppermute(blk, "seq", xor_perm(8, lambda j: j ^ 1))
    pair = jnp.concatenate([blk, sib], axis=0)
    pieces = [(blk, i, rows), (sib, i ^ 1, rows)]
    for m in (2, 4, 6):
        got = lax.ppermute(pair, "seq", xor_perm(8, lambda j, m=m: j ^ m))
        pieces += [(got[:rows], i ^ m, rows), (got[rows:], i ^ m ^ 1, rows)]
    return pieces


def project(normed, pieces, stride, offset=0):
    total = None
    for piece, source, rows in pieces:
        cols = lax.dynamic_slice_in_dim(normed, source * stride + offset, rows, 1)
        term = jnp.dot(cols, piece, preferred_element_type=jnp.float32)
        total = term if total is None else total + term
    return total


def body(
    hidden, norm_gain, w_query, w_key, w_value, doc_lengths, critic_up, critic_down, rule_ids
):
    n_seq = lax.axis_size("seq")
    n_tp = lax.axis_size("tp")
    seq_i = lax.axis_index("seq")
    tp_i = lax.axis_index("tp")
    normed = rms_norm(hidden, norm_gain)
    tokens_here = hidden.shape[0]
    d_rows = w_query.shape[0]
    heads_here = w_query.shape[1] // HEAD
    sharers = GROUP // heads_here
    kv_width = HEAD // sharers
    kv_head = tp_i * heads_here // GROUP
    kv_part = tp_i % sharers
    kv_start = kv_head * HEAD + kv_part * kv_width
    kv_weights = jnp.concatenate(
        [
            lax.dynamic_slice_in_dim(w_key, kv_start, kv_width, 1),
            lax.dynamic_slice_in_dim(w_value, kv_start, kv_width, 1),
        ],
        axis=1,
    )

    doc_ends = jnp.cumsum(doc_lengths) - 1
    first_row = seq_i * tokens_here
    query_pos = first_row + jnp.arange(tokens_here, dtype=jnp.int32)
    picker = (doc_ends[:, None] == query_pos[None, :]).astype(jnp.bfloat16)
    end_terms = jnp.dot(picker, normed, preferred_element_type=jnp.float32).astype(jnp.bfloat16)
    if n_seq == 8:
        end_rows = seq_reduce_scatter(end_terms).astype(jnp.bfloat16)
    else:
        end_rows = lax.psum_scatter(end_terms, "seq", scatter_dimension=1, tiled=True)
    up_own = jnp.dot(end_rows, critic_up, preferred_element_type=jnp.float32)
    if n_seq == 8:
        up_sum = seq_all_reduce(up_own)
    else:
        up_sum = lax.psum(up_own, "seq")
    critic_hidden = jax.nn.silu(up_sum).astype(jnp.bfloat16)
    per_rule = jnp.einsum(
        "dc,rce->dre", critic_hidden, critic_down, preferred_element_type=jnp.float32
    )
    rule_pick = rule_ids[:, None] == jnp.arange(critic_down.shape[0], dtype=jnp.int32)[None, :]
    chosen = jnp.sum(jnp.where(rule_pick[:, :, None], per_rule, 0.0), axis=1)
    if n_tp <= 8 and power_of_two(n_tp):
        critic_sum = group_sum(chosen, "tp", n_tp, n_tp, canonical=True)
    else:
        critic_sum = lax.psum(chosen, "tp")
    critic_values = critic_sum.astype(jnp.bfloat16)

    kv_pieces = gather_pieces(kv_weights, n_seq)
    kv_own = project(normed, kv_pieces, d_rows).astype(jnp.bfloat16)
    got = [kv_own] + [
        lax.ppermute(kv_own, "tp", xor_perm(n_tp, lambda j, k=k: j ^ k))
        for k in range(1, sharers)
    ]
    shares = []
    for m in range(sharers):
        value = got[0]
        for k in range(1, sharers):
            value = jnp.where((kv_part ^ k) == m, got[k], value)
        shares.append(value)
    kv_rows = jnp.concatenate(
        [v[:, :kv_width] for v in shares] + [v[:, kv_width:] for v in shares], axis=1
    )
    kv_all = gather_pieces(kv_rows, n_seq)
    key_block = jnp.concatenate([piece[:, :HEAD] for piece, _, _ in kv_all], axis=0)
    value_block = jnp.concatenate([piece[:, HEAD:] for piece, _, _ in kv_all], axis=0)
    key_pos = jnp.concatenate(
        [
            source * tokens_here + jnp.arange(piece.shape[0], dtype=jnp.int32)
            for piece, source, _ in kv_all
        ]
    )

    q_weights = lax.all_gather(w_query, "seq", axis=0, tiled=True)
    queries = (
        jnp.dot(normed, q_weights, preferred_element_type=jnp.float32)
        .astype(jnp.bfloat16)
        .reshape(tokens_here, heads_here, HEAD)
    )

    def segment_of(positions):
        return jnp.sum((positions[:, None] > doc_ends[None, :]).astype(jnp.int32), axis=1)

    query_seg = segment_of(query_pos)
    inverse_root = 1.0 / math.sqrt(HEAD)
    allowed = (query_seg[:, None] == segment_of(key_pos)[None, :]) & (
        key_pos[None, :] <= query_pos[:, None]
    )
    outs = []
    for h in range(heads_here):
        scores = (
            jnp.dot(queries[:, h, :], key_block.T, preferred_element_type=jnp.float32)
            * inverse_root
        )
        scores = jnp.where(allowed, scores, -1e30)
        maxima = jnp.max(scores, axis=1, keepdims=True)
        expanded = jnp.where(allowed, jnp.exp(scores - maxima), 0.0)
        totals = jnp.sum(expanded, axis=1, keepdims=True)
        weighted = jnp.dot(
            expanded.astype(jnp.bfloat16), value_block, preferred_element_type=jnp.float32
        )
        outs.append((weighted / totals).astype(jnp.bfloat16))
    attention = jnp.concatenate(outs, axis=1)
    return (attention, critic_values)


def solution(mesh):
    return jax.shard_map(
        body,
        mesh=mesh,
        in_specs=(
            P("seq", None),
            P(),
            P("seq", "tp"),
            P("seq", None),
            P("seq", None),
            P(),
            P("seq", "tp"),
            P(None, "tp", "seq"),
            P(),
        ),
        out_specs=(P("seq", "tp"), P(None, "seq")),
        check_vma=False,
    )
```

```python
import math

import jax
import jax.numpy as jnp
from jax import lax
from jax.sharding import PartitionSpec as P


HEAD = 128
GROUP = 8


def rms_norm(values, norm_gain):
    widened = values.astype(jnp.float32)
    mean_square = jnp.mean(widened * widened, axis=-1, keepdims=True)
    return (widened * lax.rsqrt(mean_square + 1e-05) * norm_gain.astype(jnp.float32)).astype(
        jnp.bfloat16
    )


def xor_perm(n, pick):
    return [(j, pick(j)) for j in range(n)]


def xor_all_reduce(x, axis, n):
    k = 1
    while k < n:
        x = x + lax.ppermute(x, axis, xor_perm(n, lambda j, k=k: j ^ k))
        k = k * 2
    return x


def xor_reduce_scatter(x, axis, n):
    i = lax.axis_index(axis)
    k = n // 2
    while k >= 1:
        half = x.shape[1] // 2
        bit = (i // k) % 2
        keep = lax.dynamic_slice_in_dim(x, bit * half, half, 1)
        send = lax.dynamic_slice_in_dim(x, (1 - bit) * half, half, 1)
        x = keep + lax.ppermute(send, axis, xor_perm(n, lambda j, k=k: j ^ k))
        k = k // 2
    return x


def xor_gather_stack(x, axis, n, size):
    i = lax.axis_index(axis)
    stack = x[None]
    k = 1
    while k < size:
        other = lax.ppermute(stack, axis, xor_perm(n, lambda j, k=k: j ^ k))
        low = (i // k) % 2 == 0
        stack = jnp.where(
            low,
            jnp.concatenate([stack, other], axis=0),
            jnp.concatenate([other, stack], axis=0),
        )
        k = k * 2
    return stack


def power_of_two(n):
    return n & (n - 1) == 0


def gather_pieces(blk, n):
    i = lax.axis_index("seq")
    rows = blk.shape[0]
    if n != 8:
        full = lax.all_gather(blk, "seq", axis=0, tiled=True)
        return [(full, jnp.int32(0), n * rows)]
    core = i % 2
    chip = i // 2
    sib = lax.ppermute(blk, "seq", xor_perm(8, lambda j: j ^ 1))
    pair = jnp.concatenate([blk, sib], axis=0)
    nb = lax.ppermute(pair, "seq", xor_perm(8, lambda j: j ^ 2 if j % 2 == 0 else j ^ 4))
    dg = lax.ppermute(nb[:rows], "seq", xor_perm(8, lambda j: j ^ 5 if j % 2 == 0 else j ^ 3))
    oth = lax.ppermute(jnp.concatenate([nb, dg], axis=0), "seq", xor_perm(8, lambda j: j ^ 1))
    nb_chip = chip ^ (1 + core)
    oth_chip = chip ^ (2 - core)
    diag = chip ^ 3
    return [
        (blk, i, rows),
        (sib, i ^ 1, rows),
        (nb[:rows], 2 * nb_chip + core, rows),
        (nb[rows:], 2 * nb_chip + 1 - core, rows),
        (dg, 2 * diag + 1 - core, rows),
        (oth[:rows], 2 * oth_chip + 1 - core, rows),
        (oth[rows : 2 * rows], 2 * oth_chip + core, rows),
        (oth[2 * rows :], 2 * diag + core, rows),
    ]


def project(normed, pieces):
    total = None
    for piece, source, rows in pieces:
        cols = lax.dynamic_slice_in_dim(normed, source * rows, rows, 1)
        term = jnp.dot(cols, piece, preferred_element_type=jnp.float32)
        total = term if total is None else total + term
    return total


def body(
    hidden, norm_gain, w_query, w_key, w_value, doc_lengths, critic_up, critic_down, rule_ids
):
    n_seq = lax.axis_size("seq")
    n_tp = lax.axis_size("tp")
    seq_i = lax.axis_index("seq")
    tp_i = lax.axis_index("tp")
    normed = rms_norm(hidden, norm_gain)
    tokens_here = hidden.shape[0]
    d_rows = w_query.shape[0]
    heads_here = w_query.shape[1] // HEAD
    sharers = GROUP // heads_here
    kv_width = HEAD // sharers
    kv_head = tp_i * heads_here // GROUP
    kv_part = tp_i % sharers
    kv_start = kv_head * HEAD + kv_part * kv_width
    key_cols = lax.dynamic_slice_in_dim(w_key, kv_start, kv_width, 1)
    value_cols = lax.dynamic_slice_in_dim(w_value, kv_start, kv_width, 1)
    kv_weights = jnp.concatenate([key_cols, value_cols], axis=1)

    doc_ends = jnp.cumsum(doc_lengths) - 1
    first_row = seq_i * tokens_here
    query_pos = first_row + jnp.arange(tokens_here, dtype=jnp.int32)
    picker = (doc_ends[:, None] == query_pos[None, :]).astype(jnp.bfloat16)
    end_terms = jnp.dot(picker, normed, preferred_element_type=jnp.float32).astype(jnp.bfloat16)
    if power_of_two(n_seq):
        end_rows = xor_reduce_scatter(end_terms, "seq", n_seq)
    else:
        end_rows = lax.psum_scatter(end_terms, "seq", scatter_dimension=1, tiled=True)
    up_own = jnp.dot(end_rows, critic_up, preferred_element_type=jnp.float32)
    if power_of_two(n_seq):
        up_sum = xor_all_reduce(up_own, "seq", n_seq)
    else:
        up_sum = lax.psum(up_own, "seq")
    critic_hidden = jax.nn.silu(up_sum).astype(jnp.bfloat16)
    per_rule = jnp.einsum(
        "dc,rce->dre", critic_hidden, critic_down, preferred_element_type=jnp.float32
    )
    rule_pick = rule_ids[:, None] == jnp.arange(critic_down.shape[0], dtype=jnp.int32)[None, :]
    chosen = jnp.sum(jnp.where(rule_pick[:, :, None], per_rule, 0.0), axis=1)
    if power_of_two(n_tp):
        critic_sum = xor_all_reduce(chosen, "tp", n_tp)
    else:
        critic_sum = lax.psum(chosen, "tp")
    critic_values = critic_sum.astype(jnp.bfloat16)

    kv_pieces = gather_pieces(kv_weights, n_seq)
    kv_own = project(normed, kv_pieces).astype(jnp.bfloat16)
    kv_stack = xor_gather_stack(kv_own, "tp", n_tp, sharers)
    kv_rows = jnp.concatenate(
        [kv_stack[m, :, :kv_width] for m in range(sharers)]
        + [kv_stack[m, :, kv_width:] for m in range(sharers)],
        axis=1,
    )
    kv_all = gather_pieces(kv_rows, n_seq)
    key_block = jnp.concatenate([piece[:, :HEAD] for piece, _, _ in kv_all], axis=0)
    value_block = jnp.concatenate([piece[:, HEAD:] for piece, _, _ in kv_all], axis=0)
    key_pos = jnp.concatenate(
        [
            source * tokens_here + jnp.arange(piece.shape[0], dtype=jnp.int32)
            for piece, source, _ in kv_all
        ]
    )

    if n_seq == 8:
        core = seq_i % 2
        mine = lax.all_gather(
            w_query, "seq", axis=0, tiled=True, axis_index_groups=[[0, 2, 4, 6], [1, 3, 5, 7]]
        )
        theirs = lax.ppermute(mine, "seq", xor_perm(8, lambda j: j ^ 1))
        by_core = normed.reshape(tokens_here, n_seq // 2, 2, d_rows)
        own_cols = jnp.where(core == 0, by_core[:, :, 0, :], by_core[:, :, 1, :])
        other_cols = jnp.where(core == 0, by_core[:, :, 1, :], by_core[:, :, 0, :])
        query_sum = jnp.dot(
            own_cols.reshape(tokens_here, -1), mine, preferred_element_type=jnp.float32
        ) + jnp.dot(other_cols.reshape(tokens_here, -1), theirs, preferred_element_type=jnp.float32)
    else:
        q_weights = lax.all_gather(w_query, "seq", axis=0, tiled=True)
        query_sum = jnp.dot(normed, q_weights, preferred_element_type=jnp.float32)
    queries = query_sum.astype(jnp.bfloat16).reshape(tokens_here, heads_here, HEAD)

    def segment_of(positions):
        return jnp.sum((positions[:, None] > doc_ends[None, :]).astype(jnp.int32), axis=1)

    query_seg = segment_of(query_pos)
    inverse_root = 1.0 / math.sqrt(HEAD)
    allowed = (query_seg[:, None] == segment_of(key_pos)[None, :]) & (
        key_pos[None, :] <= query_pos[:, None]
    )
    allowed = allowed[:, None, :]
    scores = (
        jnp.einsum("qhd,kd->qhk", queries, key_block, preferred_element_type=jnp.float32)
        * inverse_root
    )
    scores = jnp.where(allowed, scores, -1e30)
    maxima = jnp.max(scores, axis=2)
    expanded = jnp.where(allowed, jnp.exp(scores - maxima[:, :, None]), 0.0)
    totals = jnp.sum(expanded, axis=2)
    weighted = jnp.einsum(
        "qhk,kd->qhd",
        expanded.astype(jnp.bfloat16),
        value_block,
        preferred_element_type=jnp.float32,
    )
    attention = (
        (weighted / totals[:, :, None])
        .reshape(tokens_here, heads_here * HEAD)
        .astype(jnp.bfloat16)
    )
    return (attention, critic_values)


def solution(mesh):
    return jax.shard_map(
        body,
        mesh=mesh,
        in_specs=(
            P("seq", None),
            P(),
            P("seq", "tp"),
            P("seq", None),
            P("seq", None),
            P(),
            P("seq", "tp"),
            P(None, "tp", "seq"),
            P(),
        ),
        out_specs=(P("seq", "tp"), P(None, "seq")),
        check_vma=False,
    )
```

```python
import math

import jax
import jax.numpy as jnp
from jax import lax
from jax.sharding import PartitionSpec as P


HEAD = 128
GROUP = 8


def rms_norm(values, norm_gain):
    widened = values.astype(jnp.float32)
    mean_square = jnp.mean(widened * widened, axis=-1, keepdims=True)
    return (widened * lax.rsqrt(mean_square + 1e-05) * norm_gain.astype(jnp.float32)).astype(
        jnp.bfloat16
    )


def xor_perm(n, pick):
    return [(j, pick(j)) for j in range(n)]


def xor_all_reduce(x, axis, n):
    k = 1
    while k < n:
        x = x + lax.ppermute(x, axis, xor_perm(n, lambda j, k=k: j ^ k))
        k = k * 2
    return x


def xor_reduce_scatter(x, axis, n):
    i = lax.axis_index(axis)
    k = n // 2
    while k >= 1:
        half = x.shape[1] // 2
        bit = (i // k) % 2
        keep = lax.dynamic_slice_in_dim(x, bit * half, half, 1)
        send = lax.dynamic_slice_in_dim(x, (1 - bit) * half, half, 1)
        x = keep + lax.ppermute(send, axis, xor_perm(n, lambda j, k=k: j ^ k))
        k = k // 2
    return x


def xor_gather_stack(x, axis, n, size):
    i = lax.axis_index(axis)
    stack = x[None]
    k = 1
    while k < size:
        other = lax.ppermute(stack, axis, xor_perm(n, lambda j, k=k: j ^ k))
        low = (i // k) % 2 == 0
        stack = jnp.where(
            low,
            jnp.concatenate([stack, other], axis=0),
            jnp.concatenate([other, stack], axis=0),
        )
        k = k * 2
    return stack


def power_of_two(n):
    return n & (n - 1) == 0


def gather_pieces(blk, n):
    i = lax.axis_index("seq")
    rows = blk.shape[0]
    if n != 8:
        full = lax.all_gather(blk, "seq", axis=0, tiled=True)
        return [(full, jnp.int32(0), n * rows)]
    core = i % 2
    chip = i // 2
    sib = lax.ppermute(blk, "seq", xor_perm(8, lambda j: j ^ 1))
    pair = jnp.concatenate([blk, sib], axis=0)
    nb = lax.ppermute(pair, "seq", xor_perm(8, lambda j: j ^ 2 if j % 2 == 0 else j ^ 4))
    dg = lax.ppermute(nb[:rows], "seq", xor_perm(8, lambda j: j ^ 5 if j % 2 == 0 else j ^ 3))
    oth = lax.ppermute(jnp.concatenate([nb, dg], axis=0), "seq", xor_perm(8, lambda j: j ^ 1))
    nb_chip = chip ^ (1 + core)
    oth_chip = chip ^ (2 - core)
    diag = chip ^ 3
    return [
        (blk, i, rows),
        (sib, i ^ 1, rows),
        (nb[:rows], 2 * nb_chip + core, rows),
        (nb[rows:], 2 * nb_chip + 1 - core, rows),
        (dg, 2 * diag + 1 - core, rows),
        (oth[:rows], 2 * oth_chip + 1 - core, rows),
        (oth[rows : 2 * rows], 2 * oth_chip + core, rows),
        (oth[2 * rows :], 2 * diag + core, rows),
    ]


def body(
    hidden, norm_gain, w_query, w_key, w_value, doc_lengths, critic_up, critic_down, rule_ids
):
    n_seq = lax.axis_size("seq")
    n_tp = lax.axis_size("tp")
    seq_i = lax.axis_index("seq")
    tp_i = lax.axis_index("tp")
    normed = rms_norm(hidden, norm_gain)
    tokens_here = hidden.shape[0]
    heads_here = w_query.shape[1] // HEAD
    sharers = GROUP // heads_here
    kv_width = HEAD // sharers
    kv_head = tp_i * heads_here // GROUP
    kv_part = tp_i % sharers
    kv_start = kv_head * HEAD + kv_part * kv_width
    key_cols = lax.dynamic_slice_in_dim(w_key, kv_start, kv_width, 1)
    value_cols = lax.dynamic_slice_in_dim(w_value, kv_start, kv_width, 1)
    kv_weights = jnp.concatenate([key_cols, value_cols], axis=1)

    doc_ends = jnp.cumsum(doc_lengths) - 1
    first_row = seq_i * tokens_here
    query_pos = first_row + jnp.arange(tokens_here, dtype=jnp.int32)
    picker = (doc_ends[:, None] == query_pos[None, :]).astype(jnp.bfloat16)
    end_terms = jnp.dot(picker, normed, preferred_element_type=jnp.float32).astype(jnp.bfloat16)
    if power_of_two(n_seq):
        end_rows = xor_reduce_scatter(end_terms, "seq", n_seq)
    else:
        end_rows = lax.psum_scatter(end_terms, "seq", scatter_dimension=1, tiled=True)
    up_own = jnp.dot(end_rows, critic_up, preferred_element_type=jnp.float32)
    if power_of_two(n_seq):
        up_sum = xor_all_reduce(up_own, "seq", n_seq)
    else:
        up_sum = lax.psum(up_own, "seq")
    critic_hidden = jax.nn.silu(up_sum).astype(jnp.bfloat16)
    per_rule = jnp.einsum(
        "dc,rce->dre", critic_hidden, critic_down, preferred_element_type=jnp.float32
    )
    rule_pick = rule_ids[:, None] == jnp.arange(critic_down.shape[0], dtype=jnp.int32)[None, :]
    chosen = jnp.sum(jnp.where(rule_pick[:, :, None], per_rule, 0.0), axis=1)
    if power_of_two(n_tp):
        critic_sum = xor_all_reduce(chosen, "tp", n_tp)
    else:
        critic_sum = lax.psum(chosen, "tp")
    critic_values = critic_sum.astype(jnp.bfloat16)

    kv_full = lax.all_gather(kv_weights, "seq", axis=0, tiled=True)
    kv_own = jnp.dot(normed, kv_full, preferred_element_type=jnp.float32).astype(jnp.bfloat16)
    kv_stack = xor_gather_stack(kv_own, "tp", n_tp, sharers)
    kv_rows = jnp.concatenate(
        [kv_stack[m, :, :kv_width] for m in range(sharers)]
        + [kv_stack[m, :, kv_width:] for m in range(sharers)],
        axis=1,
    )
    kv_all = gather_pieces(kv_rows, n_seq)
    key_block = jnp.concatenate([piece[:, :HEAD] for piece, _, _ in kv_all], axis=0)
    value_block = jnp.concatenate([piece[:, HEAD:] for piece, _, _ in kv_all], axis=0)
    key_pos = jnp.concatenate(
        [
            source * tokens_here + jnp.arange(piece.shape[0], dtype=jnp.int32)
            for piece, source, _ in kv_all
        ]
    )

    q_weights = lax.all_gather(w_query, "seq", axis=0, tiled=True)
    queries = (
        jnp.dot(normed, q_weights, preferred_element_type=jnp.float32)
        .astype(jnp.bfloat16)
        .reshape(tokens_here, heads_here, HEAD)
    )

    def segment_of(positions):
        return jnp.sum((positions[:, None] > doc_ends[None, :]).astype(jnp.int32), axis=1)

    query_seg = segment_of(query_pos)
    inverse_root = 1.0 / math.sqrt(HEAD)
    allowed = (query_seg[:, None] == segment_of(key_pos)[None, :]) & (
        key_pos[None, :] <= query_pos[:, None]
    )
    allowed = allowed[:, None, :]
    scores = (
        jnp.einsum("qhd,kd->qhk", queries, key_block, preferred_element_type=jnp.float32)
        * inverse_root
    )
    scores = jnp.where(allowed, scores, -1e30)
    maxima = jnp.max(scores, axis=2)
    expanded = jnp.where(allowed, jnp.exp(scores - maxima[:, :, None]), 0.0)
    totals = jnp.sum(expanded, axis=2)
    weighted = jnp.einsum(
        "qhk,kd->qhd",
        expanded.astype(jnp.bfloat16),
        value_block,
        preferred_element_type=jnp.float32,
    )
    attention = (
        (weighted / totals[:, :, None])
        .reshape(tokens_here, heads_here * HEAD)
        .astype(jnp.bfloat16)
    )
    return (attention, critic_values)


def solution(mesh):
    return jax.shard_map(
        body,
        mesh=mesh,
        in_specs=(
            P("seq", None),
            P(),
            P("seq", "tp"),
            P("seq", None),
            P("seq", None),
            P(),
            P("seq", "tp"),
            P(None, "tp", "seq"),
            P(),
        ),
        out_specs=(P("seq", "tp"), P(None, "seq")),
        check_vma=False,
    )
```

```python
import math

import jax
import jax.numpy as jnp
from jax import lax
from jax.sharding import PartitionSpec as P


HEAD = 128
GROUP = 8


def rms_norm(values, norm_gain):
    widened = values.astype(jnp.float32)
    mean_square = jnp.mean(widened * widened, axis=-1, keepdims=True)
    return (widened * lax.rsqrt(mean_square + 1e-05) * norm_gain.astype(jnp.float32)).astype(
        jnp.bfloat16
    )


def xor_perm(n, pick):
    return [(j, pick(j)) for j in range(n)]


def seq_all_reduce(x):
    x = x + lax.ppermute(x, "seq", xor_perm(8, lambda j: j ^ 1))
    got = [lax.ppermute(x, "seq", xor_perm(8, lambda j, m=m: j ^ m)) for m in (2, 4, 6)]
    return x + got[0] + got[1] + got[2]


def seq_reduce_scatter(x):
    i = lax.axis_index("seq")
    chip_cols = x.shape[1] // 4
    own = lax.dynamic_slice_in_dim(x, (i // 2) * chip_cols, chip_cols, 1).astype(jnp.float32)
    for m in (2, 4, 6):
        part = lax.dynamic_slice_in_dim(x, ((i ^ m) // 2) * chip_cols, chip_cols, 1)
        own = own + lax.ppermute(part, "seq", xor_perm(8, lambda j, m=m: j ^ m)).astype(jnp.float32)
    half = chip_cols // 2
    core = i % 2
    keep = lax.dynamic_slice_in_dim(own, core * half, half, 1)
    send = lax.dynamic_slice_in_dim(own, (1 - core) * half, half, 1)
    return keep + lax.ppermute(send, "seq", xor_perm(8, lambda j: j ^ 1))


def group_sum(x, axis, n, size, canonical):
    got = [x] + [lax.ppermute(x, axis, xor_perm(n, lambda j, k=k: j ^ k)) for k in range(1, size)]
    if not canonical:
        total = got[0]
        for g in got[1:]:
            total = total + g
        return total
    me = lax.axis_index(axis) % size
    total = None
    for m in range(size):
        value = got[0]
        for k in range(1, size):
            value = jnp.where((me ^ k) == m, got[k], value)
        total = value if total is None else total + value
    return total


def power_of_two(n):
    return n & (n - 1) == 0


def gather_pieces(blk, n):
    i = lax.axis_index("seq")
    rows = blk.shape[0]
    if n != 8:
        full = lax.all_gather(blk, "seq", axis=0, tiled=False)
        return [(full[m], m, rows) for m in range(n)]
    sib = lax.ppermute(blk, "seq", xor_perm(8, lambda j: j ^ 1))
    pair = jnp.concatenate([blk, sib], axis=0)
    pieces = [(blk, i, rows), (sib, i ^ 1, rows)]
    for m in (2, 4, 6):
        got = lax.ppermute(pair, "seq", xor_perm(8, lambda j, m=m: j ^ m))
        pieces += [(got[:rows], i ^ m, rows), (got[rows:], i ^ m ^ 1, rows)]
    return pieces


def gather_forward(blk, n):
    i = lax.axis_index("seq")
    rows = blk.shape[0]
    if n != 8:
        full = lax.all_gather(blk, "seq", axis=0, tiled=True)
        return [(full, jnp.int32(0), n * rows)]
    core = i % 2
    chip = i // 2
    sib = lax.ppermute(blk, "seq", xor_perm(8, lambda j: j ^ 1))
    pair = jnp.concatenate([blk, sib], axis=0)
    nb = lax.ppermute(pair, "seq", xor_perm(8, lambda j: j ^ 2 if j % 2 == 0 else j ^ 4))
    dg = lax.ppermute(nb[:rows], "seq", xor_perm(8, lambda j: j ^ 5 if j % 2 == 0 else j ^ 3))
    oth = lax.ppermute(jnp.concatenate([nb, dg], axis=0), "seq", xor_perm(8, lambda j: j ^ 1))
    nb_chip = chip ^ (1 + core)
    oth_chip = chip ^ (2 - core)
    diag = chip ^ 3
    return [
        (blk, i, rows),
        (sib, i ^ 1, rows),
        (nb[:rows], 2 * nb_chip + core, rows),
        (nb[rows:], 2 * nb_chip + 1 - core, rows),
        (dg, 2 * diag + 1 - core, rows),
        (oth[:rows], 2 * oth_chip + 1 - core, rows),
        (oth[rows : 2 * rows], 2 * oth_chip + core, rows),
        (oth[2 * rows :], 2 * diag + core, rows),
    ]


def project(normed, pieces, stride, offset=0):
    total = None
    for piece, source, rows in pieces:
        cols = lax.dynamic_slice_in_dim(normed, source * stride + offset, rows, 1)
        term = jnp.dot(cols, piece, preferred_element_type=jnp.float32)
        total = term if total is None else total + term
    return total


def body(
    hidden, norm_gain, w_query, w_key, w_value, doc_lengths, critic_up, critic_down, rule_ids
):
    n_seq = lax.axis_size("seq")
    n_tp = lax.axis_size("tp")
    seq_i = lax.axis_index("seq")
    tp_i = lax.axis_index("tp")
    normed = rms_norm(hidden, norm_gain)
    tokens_here = hidden.shape[0]
    d_rows = w_query.shape[0]
    heads_here = w_query.shape[1] // HEAD
    sharers = GROUP // heads_here
    kv_width = HEAD // sharers
    kv_head = tp_i * heads_here // GROUP
    kv_part = tp_i % sharers
    kv_start = kv_head * HEAD + kv_part * kv_width
    kv_weights = jnp.concatenate(
        [
            lax.dynamic_slice_in_dim(w_key, kv_start, kv_width, 1),
            lax.dynamic_slice_in_dim(w_value, kv_start, kv_width, 1),
        ],
        axis=1,
    )

    doc_ends = jnp.cumsum(doc_lengths) - 1
    first_row = seq_i * tokens_here
    query_pos = first_row + jnp.arange(tokens_here, dtype=jnp.int32)
    picker = (doc_ends[:, None] == query_pos[None, :]).astype(jnp.bfloat16)
    picked = jnp.dot(picker, hidden, preferred_element_type=jnp.float32)
    picked_square = jnp.mean(picked * picked, axis=-1, keepdims=True)
    end_terms = (
        picked * lax.rsqrt(picked_square + 1e-05) * norm_gain.astype(jnp.float32)
    ).astype(jnp.bfloat16)
    if n_seq == 8:
        end_rows = seq_reduce_scatter(end_terms).astype(jnp.bfloat16)
    else:
        end_rows = lax.psum_scatter(end_terms, "seq", scatter_dimension=1, tiled=True)
    up_own = jnp.dot(end_rows, critic_up, preferred_element_type=jnp.float32)
    if n_seq == 8:
        up_sum = seq_all_reduce(up_own)
    else:
        up_sum = lax.psum(up_own, "seq")
    critic_hidden = jax.nn.silu(up_sum).astype(jnp.bfloat16)
    per_rule = jnp.einsum(
        "dc,rce->dre", critic_hidden, critic_down, preferred_element_type=jnp.float32
    )
    rule_pick = rule_ids[:, None] == jnp.arange(critic_down.shape[0], dtype=jnp.int32)[None, :]
    chosen = jnp.sum(jnp.where(rule_pick[:, :, None], per_rule, 0.0), axis=1)
    if n_tp <= 8 and power_of_two(n_tp):
        critic_sum = group_sum(chosen, "tp", n_tp, n_tp, canonical=True)
    else:
        critic_sum = lax.psum(chosen, "tp")
    critic_values = critic_sum.astype(jnp.bfloat16)

    kv_pieces = gather_forward(kv_weights, n_seq)
    kv_own = project(normed, kv_pieces, d_rows).astype(jnp.bfloat16)
    got = [kv_own] + [
        lax.ppermute(kv_own, "tp", xor_perm(n_tp, lambda j, k=k: j ^ k))
        for k in range(1, sharers)
    ]
    shares = []
    for m in range(sharers):
        value = got[0]
        for k in range(1, sharers):
            value = jnp.where((kv_part ^ k) == m, got[k], value)
        shares.append(value)
    kv_rows = jnp.concatenate(
        [v[:, :kv_width] for v in shares] + [v[:, kv_width:] for v in shares], axis=1
    )
    kv_all = gather_pieces(kv_rows, n_seq)
    key_block = jnp.concatenate([piece[:, :HEAD] for piece, _, _ in kv_all], axis=0)
    value_block = jnp.concatenate([piece[:, HEAD:] for piece, _, _ in kv_all], axis=0)
    key_pos = jnp.concatenate(
        [
            source * tokens_here + jnp.arange(piece.shape[0], dtype=jnp.int32)
            for piece, source, _ in kv_all
        ]
    )

    q_weights = lax.all_gather(w_query, "seq", axis=0, tiled=True)
    queries = (
        jnp.dot(normed, q_weights, preferred_element_type=jnp.float32)
        .astype(jnp.bfloat16)
        .reshape(tokens_here, heads_here, HEAD)
    )

    def segment_of(positions):
        return jnp.sum((positions[:, None] > doc_ends[None, :]).astype(jnp.int32), axis=1)

    query_seg = segment_of(query_pos)
    allowed = (query_seg[:, None] == segment_of(key_pos)[None, :]) & (
        key_pos[None, :] <= query_pos[:, None]
    )
    attention = attend(queries, key_block, value_block, allowed, heads_here)
    return (attention, critic_values)


def attend(queries, key_block, value_block, allowed, heads_here):
    inverse_root = 1.0 / math.sqrt(HEAD)
    outs = []
    for h in range(heads_here):
        scores = (
            jnp.dot(queries[:, h, :], key_block.T, preferred_element_type=jnp.float32)
            * inverse_root
        )
        scores = jnp.where(allowed, scores, -1e30)
        maxima = jnp.max(scores, axis=1, keepdims=True)
        expanded = jnp.where(allowed, jnp.exp(scores - maxima), 0.0)
        totals = jnp.sum(expanded, axis=1, keepdims=True)
        weighted = jnp.dot(
            expanded.astype(jnp.bfloat16), value_block, preferred_element_type=jnp.float32
        )
        outs.append((weighted / totals).astype(jnp.bfloat16))
    return jnp.concatenate(outs, axis=1)


def solution(mesh):
    return jax.shard_map(
        body,
        mesh=mesh,
        in_specs=(
            P("seq", None),
            P(),
            P("seq", "tp"),
            P("seq", None),
            P("seq", None),
            P(),
            P("seq", "tp"),
            P(None, "tp", "seq"),
            P(),
        ),
        out_specs=(P("seq", "tp"), P(None, "seq")),
        check_vma=False,
    )
```

```python
import math

import jax
import jax.numpy as jnp
from jax import lax
from jax.sharding import PartitionSpec as P


HEAD = 128
GROUP = 8


def rms_norm(values, norm_gain):
    widened = values.astype(jnp.float32)
    mean_square = jnp.mean(widened * widened, axis=-1, keepdims=True)
    return (widened * lax.rsqrt(mean_square + 1e-05) * norm_gain.astype(jnp.float32)).astype(
        jnp.bfloat16
    )


def xor_perm(n, pick):
    return [(j, pick(j)) for j in range(n)]


def seq_all_reduce(x):
    x = x + lax.ppermute(x, "seq", xor_perm(8, lambda j: j ^ 1))
    got = [lax.ppermute(x, "seq", xor_perm(8, lambda j, m=m: j ^ m)) for m in (2, 4, 6)]
    return x + got[0] + got[1] + got[2]


def seq_reduce_scatter(x):
    i = lax.axis_index("seq")
    chip_cols = x.shape[1] // 4
    own = lax.dynamic_slice_in_dim(x, (i // 2) * chip_cols, chip_cols, 1).astype(jnp.float32)
    for m in (2, 4, 6):
        part = lax.dynamic_slice_in_dim(x, ((i ^ m) // 2) * chip_cols, chip_cols, 1)
        own = own + lax.ppermute(part, "seq", xor_perm(8, lambda j, m=m: j ^ m)).astype(jnp.float32)
    half = chip_cols // 2
    core = i % 2
    keep = lax.dynamic_slice_in_dim(own, core * half, half, 1)
    send = lax.dynamic_slice_in_dim(own, (1 - core) * half, half, 1)
    return keep + lax.ppermute(send, "seq", xor_perm(8, lambda j: j ^ 1))


def group_sum(x, axis, n, size, canonical):
    got = [x] + [lax.ppermute(x, axis, xor_perm(n, lambda j, k=k: j ^ k)) for k in range(1, size)]
    if not canonical:
        total = got[0]
        for g in got[1:]:
            total = total + g
        return total
    me = lax.axis_index(axis) % size
    total = None
    for m in range(size):
        value = got[0]
        for k in range(1, size):
            value = jnp.where((me ^ k) == m, got[k], value)
        total = value if total is None else total + value
    return total


def power_of_two(n):
    return n & (n - 1) == 0


def gather_pieces(blk, n):
    i = lax.axis_index("seq")
    rows = blk.shape[0]
    if n != 8:
        full = lax.all_gather(blk, "seq", axis=0, tiled=False)
        return [(full[m], m, rows) for m in range(n)]
    sib = lax.ppermute(blk, "seq", xor_perm(8, lambda j: j ^ 1))
    pair = jnp.concatenate([blk, sib], axis=0)
    pieces = [(blk, i, rows), (sib, i ^ 1, rows)]
    for m in (2, 4, 6):
        got = lax.ppermute(pair, "seq", xor_perm(8, lambda j, m=m: j ^ m))
        pieces += [(got[:rows], i ^ m, rows), (got[rows:], i ^ m ^ 1, rows)]
    return pieces


def gather_forward(blk, n):
    i = lax.axis_index("seq")
    rows = blk.shape[0]
    if n != 8:
        full = lax.all_gather(blk, "seq", axis=0, tiled=True)
        return [(full, jnp.int32(0), n * rows)]
    core = i % 2
    chip = i // 2
    sib = lax.ppermute(blk, "seq", xor_perm(8, lambda j: j ^ 1))
    pair = jnp.concatenate([blk, sib], axis=0)
    nb = lax.ppermute(pair, "seq", xor_perm(8, lambda j: j ^ 2 if j % 2 == 0 else j ^ 4))
    dg = lax.ppermute(nb[:rows], "seq", xor_perm(8, lambda j: j ^ 5 if j % 2 == 0 else j ^ 3))
    oth = lax.ppermute(jnp.concatenate([nb, dg], axis=0), "seq", xor_perm(8, lambda j: j ^ 1))
    nb_chip = chip ^ (1 + core)
    oth_chip = chip ^ (2 - core)
    diag = chip ^ 3
    return [
        (blk, i, rows),
        (sib, i ^ 1, rows),
        (nb[:rows], 2 * nb_chip + core, rows),
        (nb[rows:], 2 * nb_chip + 1 - core, rows),
        (dg, 2 * diag + 1 - core, rows),
        (oth[:rows], 2 * oth_chip + 1 - core, rows),
        (oth[rows : 2 * rows], 2 * oth_chip + core, rows),
        (oth[2 * rows :], 2 * diag + core, rows),
    ]


def project(normed, pieces, stride, offset=0):
    total = None
    for piece, source, rows in pieces:
        cols = lax.dynamic_slice_in_dim(normed, source * stride + offset, rows, 1)
        term = jnp.dot(cols, piece, preferred_element_type=jnp.float32)
        total = term if total is None else total + term
    return total


def body(
    hidden, norm_gain, w_query, w_key, w_value, doc_lengths, critic_up, critic_down, rule_ids
):
    n_seq = lax.axis_size("seq")
    n_tp = lax.axis_size("tp")
    seq_i = lax.axis_index("seq")
    tp_i = lax.axis_index("tp")
    normed = rms_norm(hidden, norm_gain)
    tokens_here = hidden.shape[0]
    d_rows = w_query.shape[0]
    heads_here = w_query.shape[1] // HEAD
    sharers = GROUP // heads_here
    kv_width = HEAD // sharers
    kv_head = tp_i * heads_here // GROUP
    kv_part = tp_i % sharers
    kv_start = kv_head * HEAD + kv_part * kv_width
    kv_weights = None
    for start in range(0, w_key.shape[1], kv_width):
        option = jnp.concatenate(
            [w_key[:, start : start + kv_width], w_value[:, start : start + kv_width]], axis=1
        )
        kv_weights = option if kv_weights is None else jnp.where(kv_start == start, option, kv_weights)

    doc_ends = jnp.cumsum(doc_lengths) - 1
    first_row = seq_i * tokens_here
    query_pos = first_row + jnp.arange(tokens_here, dtype=jnp.int32)
    picker = (doc_ends[:, None] == query_pos[None, :]).astype(jnp.bfloat16)
    end_terms = jnp.dot(picker, normed, preferred_element_type=jnp.float32).astype(jnp.bfloat16)
    if n_seq == 8:
        end_rows = seq_reduce_scatter(end_terms).astype(jnp.bfloat16)
    else:
        end_rows = lax.psum_scatter(end_terms, "seq", scatter_dimension=1, tiled=True)
    up_own = jnp.dot(end_rows, critic_up, preferred_element_type=jnp.float32)
    if n_seq == 8:
        up_sum = seq_all_reduce(up_own)
    else:
        up_sum = lax.psum(up_own, "seq")
    critic_hidden = jax.nn.silu(up_sum).astype(jnp.bfloat16)
    per_rule = jnp.einsum(
        "dc,rce->dre", critic_hidden, critic_down, preferred_element_type=jnp.float32
    )
    rule_pick = rule_ids[:, None] == jnp.arange(critic_down.shape[0], dtype=jnp.int32)[None, :]
    chosen = jnp.sum(jnp.where(rule_pick[:, :, None], per_rule, 0.0), axis=1)
    if n_tp <= 8 and power_of_two(n_tp):
        critic_sum = group_sum(chosen, "tp", n_tp, n_tp, canonical=True)
    else:
        critic_sum = lax.psum(chosen, "tp")
    critic_values = critic_sum.astype(jnp.bfloat16)

    kv_pieces = gather_forward(kv_weights, n_seq)
    kv_own = project(normed, kv_pieces, d_rows).astype(jnp.bfloat16)
    got = [kv_own] + [
        lax.ppermute(kv_own, "tp", xor_perm(n_tp, lambda j, k=k: j ^ k))
        for k in range(1, sharers)
    ]
    shares = []
    for m in range(sharers):
        value = got[0]
        for k in range(1, sharers):
            value = jnp.where((kv_part ^ k) == m, got[k], value)
        shares.append(value)
    kv_rows = jnp.concatenate(
        [v[:, :kv_width] for v in shares] + [v[:, kv_width:] for v in shares], axis=1
    )
    kv_all = gather_pieces(kv_rows, n_seq)
    key_block = jnp.concatenate([piece[:, :HEAD] for piece, _, _ in kv_all], axis=0)
    value_block = jnp.concatenate([piece[:, HEAD:] for piece, _, _ in kv_all], axis=0)
    key_pos = jnp.concatenate(
        [
            source * tokens_here + jnp.arange(piece.shape[0], dtype=jnp.int32)
            for piece, source, _ in kv_all
        ]
    )

    q_weights = lax.all_gather(w_query, "seq", axis=0, tiled=True)
    queries = (
        jnp.dot(normed, q_weights, preferred_element_type=jnp.float32)
        .astype(jnp.bfloat16)
        .reshape(tokens_here, heads_here, HEAD)
    )

    def segment_of(positions):
        return jnp.sum((positions[:, None] > doc_ends[None, :]).astype(jnp.int32), axis=1)

    query_seg = segment_of(query_pos)
    allowed = (query_seg[:, None] == segment_of(key_pos)[None, :]) & (
        key_pos[None, :] <= query_pos[:, None]
    )
    attention = attend(queries, key_block, value_block, allowed, heads_here)
    return (attention, critic_values)


def attend(queries, key_block, value_block, allowed, heads_here):
    inverse_root = 1.0 / math.sqrt(HEAD)
    outs = []
    for h in range(heads_here):
        scores = (
            jnp.dot(queries[:, h, :], key_block.T, preferred_element_type=jnp.float32)
            * inverse_root
        )
        scores = jnp.where(allowed, scores, -1e30)
        maxima = jnp.max(scores, axis=1, keepdims=True)
        expanded = jnp.where(allowed, jnp.exp(scores - maxima), 0.0)
        totals = jnp.sum(expanded, axis=1, keepdims=True)
        weighted = jnp.dot(
            expanded.astype(jnp.bfloat16), value_block, preferred_element_type=jnp.float32
        )
        outs.append((weighted / totals).astype(jnp.bfloat16))
    return jnp.concatenate(outs, axis=1)


def solution(mesh):
    return jax.shard_map(
        body,
        mesh=mesh,
        in_specs=(
            P("seq", None),
            P(),
            P("seq", "tp"),
            P("seq", None),
            P("seq", None),
            P(),
            P("seq", "tp"),
            P(None, "tp", "seq"),
            P(),
        ),
        out_specs=(P("seq", "tp"), P(None, "seq")),
        check_vma=False,
    )
```

```python
import math

import jax
import jax.numpy as jnp
from jax import lax
from jax.sharding import PartitionSpec as P


HEAD = 128
GROUP = 8


def rms_norm(values, norm_gain):
    widened = values.astype(jnp.float32)
    mean_square = jnp.mean(widened * widened, axis=-1, keepdims=True)
    return (widened * lax.rsqrt(mean_square + 1e-05) * norm_gain.astype(jnp.float32)).astype(
        jnp.bfloat16
    )


def xor_perm(n, pick):
    return [(j, pick(j)) for j in range(n)]


def seq_all_reduce(x):
    x = x + lax.ppermute(x, "seq", xor_perm(8, lambda j: j ^ 1))
    got = [lax.ppermute(x, "seq", xor_perm(8, lambda j, m=m: j ^ m)) for m in (2, 4, 6)]
    return x + got[0] + got[1] + got[2]


def seq_reduce_scatter(x):
    i = lax.axis_index("seq")
    chip_cols = x.shape[1] // 4
    own = lax.dynamic_slice_in_dim(x, (i // 2) * chip_cols, chip_cols, 1).astype(jnp.float32)
    for m in (2, 4, 6):
        part = lax.dynamic_slice_in_dim(x, ((i ^ m) // 2) * chip_cols, chip_cols, 1)
        own = own + lax.ppermute(part, "seq", xor_perm(8, lambda j, m=m: j ^ m)).astype(jnp.float32)
    half = chip_cols // 2
    core = i % 2
    keep = lax.dynamic_slice_in_dim(own, core * half, half, 1)
    send = lax.dynamic_slice_in_dim(own, (1 - core) * half, half, 1)
    return keep + lax.ppermute(send, "seq", xor_perm(8, lambda j: j ^ 1))


def group_sum(x, axis, n, size, canonical):
    got = [x] + [lax.ppermute(x, axis, xor_perm(n, lambda j, k=k: j ^ k)) for k in range(1, size)]
    if not canonical:
        total = got[0]
        for g in got[1:]:
            total = total + g
        return total
    me = lax.axis_index(axis) % size
    total = None
    for m in range(size):
        value = got[0]
        for k in range(1, size):
            value = jnp.where((me ^ k) == m, got[k], value)
        total = value if total is None else total + value
    return total


def power_of_two(n):
    return n & (n - 1) == 0


def gather_pieces(blk, n):
    i = lax.axis_index("seq")
    rows = blk.shape[0]
    if n != 8:
        full = lax.all_gather(blk, "seq", axis=0, tiled=False)
        return [(full[m], m, rows) for m in range(n)]
    sib = lax.ppermute(blk, "seq", xor_perm(8, lambda j: j ^ 1))
    pair = jnp.concatenate([blk, sib], axis=0)
    pieces = [(blk, i, rows), (sib, i ^ 1, rows)]
    for m in (2, 4, 6):
        got = lax.ppermute(pair, "seq", xor_perm(8, lambda j, m=m: j ^ m))
        pieces += [(got[:rows], i ^ m, rows), (got[rows:], i ^ m ^ 1, rows)]
    return pieces


def gather_forward(blk, n):
    i = lax.axis_index("seq")
    rows = blk.shape[0]
    if n != 8:
        full = lax.all_gather(blk, "seq", axis=0, tiled=True)
        return [(full, jnp.int32(0), n * rows)]
    core = i % 2
    chip = i // 2
    sib = lax.ppermute(blk, "seq", xor_perm(8, lambda j: j ^ 1))
    pair = jnp.concatenate([blk, sib], axis=0)
    nb = lax.ppermute(pair, "seq", xor_perm(8, lambda j: j ^ 2 if j % 2 == 0 else j ^ 4))
    dg = lax.ppermute(nb[:rows], "seq", xor_perm(8, lambda j: j ^ 5 if j % 2 == 0 else j ^ 3))
    oth = lax.ppermute(jnp.concatenate([nb, dg], axis=0), "seq", xor_perm(8, lambda j: j ^ 1))
    nb_chip = chip ^ (1 + core)
    oth_chip = chip ^ (2 - core)
    diag = chip ^ 3
    return [
        (blk, i, rows),
        (sib, i ^ 1, rows),
        (nb[:rows], 2 * nb_chip + core, rows),
        (nb[rows:], 2 * nb_chip + 1 - core, rows),
        (dg, 2 * diag + 1 - core, rows),
        (oth[:rows], 2 * oth_chip + 1 - core, rows),
        (oth[rows : 2 * rows], 2 * oth_chip + core, rows),
        (oth[2 * rows :], 2 * diag + core, rows),
    ]


def project(normed, pieces, stride, offset=0):
    total = None
    for piece, source, rows in pieces:
        cols = lax.dynamic_slice_in_dim(normed, source * stride + offset, rows, 1)
        term = jnp.dot(cols, piece, preferred_element_type=jnp.float32)
        total = term if total is None else total + term
    return total


def body(
    hidden, norm_gain, w_query, w_key, w_value, doc_lengths, critic_up, critic_down, rule_ids
):
    n_seq = lax.axis_size("seq")
    n_tp = lax.axis_size("tp")
    seq_i = lax.axis_index("seq")
    tp_i = lax.axis_index("tp")
    normed = rms_norm(hidden, norm_gain)
    tokens_here = hidden.shape[0]
    d_rows = w_query.shape[0]
    heads_here = w_query.shape[1] // HEAD
    sharers = GROUP // heads_here
    kv_width = HEAD // sharers
    kv_head = tp_i * heads_here // GROUP
    kv_part = tp_i % sharers
    kv_start = kv_head * HEAD + kv_part * kv_width
    kv_weights = jnp.concatenate(
        [
            lax.dynamic_slice_in_dim(w_key, kv_start, kv_width, 1),
            lax.dynamic_slice_in_dim(w_value, kv_start, kv_width, 1),
        ],
        axis=1,
    )

    doc_ends = jnp.cumsum(doc_lengths) - 1
    first_row = seq_i * tokens_here
    query_pos = first_row + jnp.arange(tokens_here, dtype=jnp.int32)
    picker = (doc_ends[:, None] == query_pos[None, :]).astype(jnp.bfloat16)
    end_terms = jnp.dot(picker, normed, preferred_element_type=jnp.float32).astype(jnp.bfloat16)
    if n_seq == 8:
        end_rows = seq_reduce_scatter(end_terms).astype(jnp.bfloat16)
    else:
        end_rows = lax.psum_scatter(end_terms, "seq", scatter_dimension=1, tiled=True)
    up_own = jnp.dot(end_rows, critic_up, preferred_element_type=jnp.float32)
    if n_seq == 8:
        up_sum = seq_all_reduce(up_own)
    else:
        up_sum = lax.psum(up_own, "seq")
    critic_hidden = jax.nn.silu(up_sum).astype(jnp.bfloat16)
    per_rule = jnp.einsum(
        "dc,rce->dre", critic_hidden, critic_down, preferred_element_type=jnp.float32
    )
    rule_pick = rule_ids[:, None] == jnp.arange(critic_down.shape[0], dtype=jnp.int32)[None, :]
    chosen = jnp.sum(jnp.where(rule_pick[:, :, None], per_rule, 0.0), axis=1)
    if n_tp <= 8 and power_of_two(n_tp):
        critic_sum = group_sum(chosen, "tp", n_tp, n_tp, canonical=True)
    else:
        critic_sum = lax.psum(chosen, "tp")
    critic_values = critic_sum.astype(jnp.bfloat16)

    kv_pieces = gather_forward(kv_weights, n_seq)
    kv_own = project(normed, kv_pieces, d_rows).astype(jnp.bfloat16)
    got = [kv_own] + [
        lax.ppermute(kv_own, "tp", xor_perm(n_tp, lambda j, k=k: j ^ k))
        for k in range(1, sharers)
    ]
    shares = []
    for m in range(sharers):
        value = got[0]
        for k in range(1, sharers):
            value = jnp.where((kv_part ^ k) == m, got[k], value)
        shares.append(value)
    kv_rows = jnp.concatenate(
        [v[:, :kv_width] for v in shares] + [v[:, kv_width:] for v in shares], axis=1
    )
    kv_all = gather_pieces(kv_rows, n_seq)
    key_block = jnp.concatenate([piece[:, :HEAD] for piece, _, _ in kv_all], axis=0)
    value_block = jnp.concatenate([piece[:, HEAD:] for piece, _, _ in kv_all], axis=0)
    key_pos = jnp.concatenate(
        [
            source * tokens_here + jnp.arange(piece.shape[0], dtype=jnp.int32)
            for piece, source, _ in kv_all
        ]
    )

    q_weights = lax.all_gather(w_query, "seq", axis=0, tiled=True)
    queries = (
        jnp.dot(normed, q_weights, preferred_element_type=jnp.float32)
        .astype(jnp.bfloat16)
        .reshape(tokens_here, heads_here, HEAD)
    )

    def segment_of(positions):
        return jnp.sum((positions[:, None] > doc_ends[None, :]).astype(jnp.int32), axis=1)

    query_seg = segment_of(query_pos)
    allowed = (query_seg[:, None] == segment_of(key_pos)[None, :]) & (
        key_pos[None, :] <= query_pos[:, None]
    )
    attention = attend(queries, key_block, value_block, allowed, heads_here)
    return (attention, critic_values)


def attend(queries, key_block, value_block, allowed, heads_here):
    inverse_root = 1.0 / math.sqrt(HEAD)
    outs = []
    for h in range(heads_here):
        scores = (
            jnp.dot(queries[:, h, :], key_block.T, preferred_element_type=jnp.float32)
            * inverse_root
        )
        scores = jnp.where(allowed, scores, -1e30)
        maxima = jnp.max(scores, axis=1, keepdims=True)
        expanded = jnp.where(allowed, jnp.exp(scores - maxima), 0.0)
        totals = jnp.sum(expanded, axis=1, keepdims=True)
        weighted = jnp.dot(
            expanded.astype(jnp.bfloat16), value_block, preferred_element_type=jnp.float32
        )
        outs.append((weighted / totals).astype(jnp.bfloat16))
    return jnp.concatenate(outs, axis=1)


def solution(mesh):
    return jax.shard_map(
        body,
        mesh=mesh,
        in_specs=(
            P("seq", None),
            P(),
            P("seq", "tp"),
            P("seq", None),
            P("seq", None),
            P(),
            P("seq", "tp"),
            P(None, "tp", "seq"),
            P(),
        ),
        out_specs=(P("seq", "tp"), P(None, "seq")),
        check_vma=False,
    )
```
